32 devices in a mesh: inner: 2 (over y), outer: 16 (over z, x, core).
Axes of the slice: x: 2, y: 2, z: 4, core: 2. Of those that a mesh axis runs over, the one named last changes fastest.
Arguments:
- propagator_matrices: bfloat16 [16, 48, 256, 256], P('outer', 'inner')
- smoothed_adjoints: float32 [16, 48, 256], P('outer', 'inner'), may hold values from -0.4330127 to 0.4330127
- station_loadings: float32 [16, 48, 2, 128], P('outer', 'inner'), may hold values from -0.21650635 to 0.21650635
- offset_response: float32 [16, 48, 256], P('outer', 'inner'), may hold values from -0.021650635 to 0.021650635
Outputs:
- adjoint: float32 [16, 48, 256], P('outer', 'inner')
- spatial_matrix_derivative: float32 [128, 128], replicated
- variance_derivative: float32 [], replicated
The draws below stay inside these ranges and needn't reach their ends.
All inputs are finite; a program needn't handle non-finite values.
Results may differ from the reference program's by a relative error of at most 0.0003.
Values sent between devices are 32-bit elements; how exact they have to be, the bound alone decides.
No kernel may reach another device: no remote copies, remote signals or barrier semaphores. Data moves between devices by JAX's collectives and lax.ppermute only.
A program may use at most 128 MiB of HBM per device.

```python
import math
import jax
import jax.numpy as jnp
from jax import lax

STATION_NUMBER = 128
STATE_LENGTH = 256
MOMENT_BATCHES = 16
MOMENTS_IN_BATCH = 48
MOMENTS_OVERALL = 768


def draw_propagator_matrices(key, part):
    choosing_seed, steady_random_start, quick_seed, shift_random_start, impulse_random_start, tier_random_start, upset_random_start = jax.random.split(key, 7)
    share = 0.5
    pick = jax.random.uniform(choosing_seed, (STATE_LENGTH,), jnp.float32) < share
    unhurried = jnp.exp(jax.random.uniform(steady_random_start, (STATE_LENGTH,), jnp.float32, math.log(0.05), math.log(0.8))) / MOMENTS_OVERALL
    fast = jnp.exp(jax.random.uniform(quick_seed, (STATE_LENGTH,), jnp.float32, math.log(0.02), math.log(0.7)))
    rates = jnp.where(pick, unhurried, fast)
    diagonal_boost = jnp.exp(jax.random.uniform(shift_random_start, (MOMENT_BATCHES, MOMENTS_IN_BATCH, STATE_LENGTH), jnp.float32, -0.35, 0.35))
    consistent_number = jax.random.randint(impulse_random_start, (MOMENT_BATCHES, MOMENTS_IN_BATCH, 1), 0, MOMENTS_OVERALL) < 3
    nesting_level = jax.random.uniform(tier_random_start, (MOMENT_BATCHES, MOMENTS_IN_BATCH, 1), jnp.float32, 0.5, 0.8)
    factor = jnp.where(consistent_number, nesting_level, 1.0).astype(jnp.float32)
    rowscale = jnp.exp(-rates[None, None, :] * diagonal_boost) * factor
    measurement_variance = jax.random.normal(upset_random_start, (MOMENT_BATCHES, MOMENTS_IN_BATCH, STATE_LENGTH, STATE_LENGTH), jnp.float32) * math.sqrt(3.0 / (MOMENTS_OVERALL * STATE_LENGTH))
    whole = (jnp.eye(STATE_LENGTH, dtype=jnp.float32) + measurement_variance) * rowscale[..., :, None]
    return whole.astype(jnp.bfloat16)


def block_scale(key, shape, cuts, smallest, top_value):
    gain, own = 1.0, jax.random.fold_in(key, 6)
    for axis_at, blocks in cuts:
        draws = jnp.exp(jax.random.uniform(jax.random.fold_in(own, axis_at), (blocks,), jnp.float32, smallest / len(cuts), top_value / len(cuts)))
        gain = gain * jnp.repeat(draws, shape[axis_at] // blocks).reshape([-1 if axis == axis_at else 1 for axis in range(len(shape))])
    return gain


def bell_draw(stream_key, dims, width, most, cuts=(), kind=jnp.bfloat16):
    array = jax.random.normal(stream_key, dims, jnp.float32) * width
    if len(cuts) > 0:
        array = block_scale(stream_key, dims, cuts, -0.22, 0.18) * array
    return jnp.clip(array, min=-most, max=most).astype(kind)


def setup_inputs(seed: int = 0) -> dict:
    splits = jax.random.split(jax.random.key(seed), 5)
    propagator_matrices = draw_propagator_matrices(jax.random.fold_in(splits[4], 71), 0)
    smoothed_adjoints = bell_draw(splits[1], (MOMENT_BATCHES, MOMENTS_IN_BATCH, STATE_LENGTH), (2.0 * MOMENTS_OVERALL ** -0.5), 0.4330127, ((0, 16), (1, 2)), jnp.float32)
    station_loadings = bell_draw(splits[2], (MOMENT_BATCHES, MOMENTS_IN_BATCH, 2, STATION_NUMBER), (1.0 * MOMENTS_OVERALL ** -0.5), 0.21650635, ((0, 16), (1, 2)), jnp.float32)
    offset_response = bell_draw(splits[3], (MOMENT_BATCHES, MOMENTS_IN_BATCH, STATE_LENGTH), (0.1 * MOMENTS_OVERALL ** -0.5), 0.021650635, ((0, 16), (1, 2)), jnp.float32)
    return dict(propagator_matrices=propagator_matrices, smoothed_adjoints=smoothed_adjoints, station_loadings=station_loadings, offset_response=offset_response)


def reference(propagator_matrices, smoothed_adjoints, station_loadings, offset_response):
    matrix_list = propagator_matrices.reshape(MOMENTS_OVERALL, STATE_LENGTH, STATE_LENGTH)
    derivative_results = smoothed_adjoints.reshape(MOMENTS_OVERALL, STATE_LENGTH)

    def backward(carry, items):
        matrix, grad_row = items
        lam = grad_row + carry
        message = jnp.dot(lam, matrix.astype(jnp.float32), precision=lax.Precision.HIGHEST)
        return message, lam

    _, length_rates = lax.scan(backward, jnp.zeros((STATE_LENGTH,), jnp.float32), (matrix_list, derivative_results), reverse=True)
    argument_values = station_loadings.reshape(MOMENTS_OVERALL, 2, STATION_NUMBER)
    spatial_matrix_derivative = jnp.dot(length_rates[:, :STATION_NUMBER].T, argument_values[:, 0, :], precision=lax.Precision.HIGHEST)
    spatial_matrix_derivative = spatial_matrix_derivative + jnp.dot(length_rates[:, STATION_NUMBER:].T, argument_values[:, 1, :], precision=lax.Precision.HIGHEST)
    variance_derivative = -jnp.sum(length_rates * offset_response.reshape(MOMENTS_OVERALL, STATE_LENGTH))
    return (length_rates.reshape(MOMENT_BATCHES, MOMENTS_IN_BATCH, STATE_LENGTH), spatial_matrix_derivative, variance_derivative)
```

```python
import jax
import jax.numpy as jnp
from jax import lax
from jax.sharding import PartitionSpec as P

EXACT = lax.Precision.HIGHEST
AXES = ("inner", "outer")


def vecmat(v, q):
    return jnp.einsum("nj,njk->nk", v, q.astype(jnp.float32), precision=EXACT)


def matmat(later, earlier):
    if later.dtype == jnp.bfloat16 and earlier.dtype == jnp.bfloat16:
        return jnp.einsum("nij,njk->nik", later, earlier, preferred_element_type=jnp.float32)
    return jnp.einsum(
        "nij,njk->nik", later.astype(jnp.float32), earlier.astype(jnp.float32), precision=EXACT
    )


def upsweep(q, v):
    levels = [(q, v)]
    while q.shape[0] > 1:
        n = q.shape[0]
        half = n // 2
        qa, qb = q[0 : 2 * half : 2], q[1 : 2 * half : 2]
        va, vb = v[0 : 2 * half : 2], v[1 : 2 * half : 2]
        nq = matmat(qb, qa)
        nv = vecmat(vb, qa) + va
        if n % 2:
            nq = jnp.concatenate([nq, q[-1:].astype(jnp.float32)], axis=0)
            nv = jnp.concatenate([nv, v[-1:]], axis=0)
        q, v = nq, nv
        levels.append((q, v))
    return levels


def downsweep(levels, incoming):
    m = incoming
    for q, v in reversed(levels[:-1]):
        n = q.shape[0]
        half = n // 2
        top = m[:half]
        left = vecmat(top, q[1 : 2 * half : 2]) + v[1 : 2 * half : 2]
        m_new = jnp.stack([left, top], axis=1).reshape(2 * half, -1)
        if n % 2:
            m_new = jnp.concatenate([m_new, m[-1:]], axis=0)
        m = m_new
    return m


def place(b):
    inner = lax.axis_size("inner")
    return (b % inner) * lax.axis_size("outer") + b // inner


def shift_from_later(x, d, count):
    return lax.ppermute(x, AXES, [(place(j + d), place(j)) for j in range(count - d)])


def body(propagator_matrices, smoothed_adjoints, station_loadings, offset_response):
    blocks = propagator_matrices[0]
    grads = smoothed_adjoints[0]
    stations = station_loadings.shape[3]
    count = lax.axis_size("outer") * lax.axis_size("inner")
    me = lax.axis_index("outer") * lax.axis_size("inner") + lax.axis_index("inner")

    leaf_v = vecmat(grads, blocks)
    levels = upsweep(blocks, leaf_v)
    q, v = levels[-1]
    q, v = q[0].astype(jnp.float32), v[0]

    span = 1
    while 2 * span < count:
        rq, rv = shift_from_later((q, v), span, count)
        valid = me + span < count
        nq = jnp.dot(rq, q, precision=EXACT)
        nv = jnp.dot(rv, q, precision=EXACT) + v
        q = jnp.where(valid, nq, q)
        v = jnp.where(valid, nv, v)
        span *= 2
    rv = shift_from_later(v, span, count)
    w = jnp.where(me + span < count, jnp.dot(rv, q, precision=EXACT) + v, v)
    incoming = shift_from_later(w, 1, count)
    incoming = jnp.where(me + 1 < count, incoming, jnp.zeros_like(incoming))

    after = downsweep(levels, incoming[None, :])
    length_rates = grads + after
    argument_values = station_loadings[0]
    local_kernel = jnp.dot(
        length_rates[:, :stations].T, argument_values[:, 0, :], precision=EXACT
    )
    local_kernel = local_kernel + jnp.dot(
        length_rates[:, stations:].T, argument_values[:, 1, :], precision=EXACT
    )
    local_noise = -jnp.sum(length_rates * offset_response[0])
    noise_row = jnp.zeros((1, local_kernel.shape[1]), jnp.float32).at[0, 0].set(local_noise)
    packed = jnp.concatenate([local_kernel, noise_row], axis=0)
    d = 1
    while d < count:
        packed = packed + lax.ppermute(packed, AXES, [(place(j), place(j ^ d)) for j in range(count)])
        d *= 2
    return (length_rates[None], packed[:stations], packed[stations, 0])


def solution(mesh):
    return jax.shard_map(
        body,
        mesh=mesh,
        in_specs=(
            P("outer", "inner", None, None),
            P("outer", "inner", None),
            P("outer", "inner", None, None),
            P("outer", "inner", None),
        ),
        out_specs=(P("outer", "inner", None), P(), P()),
        check_vma=False,
    )
```

```python
import jax
import jax.numpy as jnp
from jax import lax
from jax.sharding import PartitionSpec as P

EXACT = lax.Precision.HIGHEST
AXES = ("inner", "outer")


def vecmat(v, q):
    return jnp.sum(v[:, :, None] * q.astype(jnp.float32), axis=1)


def matmat(later, earlier):
    if later.dtype == jnp.bfloat16 and earlier.dtype == jnp.bfloat16:
        return jnp.einsum("nij,njk->nik", later, earlier, preferred_element_type=jnp.float32)
    return jnp.einsum(
        "nij,njk->nik", later.astype(jnp.float32), earlier.astype(jnp.float32), precision=EXACT
    )


def upsweep(q, v):
    levels = [(q, v)]
    while q.shape[0] > 1:
        n = q.shape[0]
        half = n // 2
        qa, qb = q[0 : 2 * half : 2], q[1 : 2 * half : 2]
        va, vb = v[0 : 2 * half : 2], v[1 : 2 * half : 2]
        nq = matmat(qb, qa)
        nv = vecmat(vb, qa) + va
        if n % 2:
            nq = jnp.concatenate([nq, q[-1:].astype(jnp.float32)], axis=0)
            nv = jnp.concatenate([nv, v[-1:]], axis=0)
        q, v = nq, nv
        levels.append((q, v))
    return levels


def downsweep(levels, top):
    m = top
    width = top.shape[2]
    offset_row = jnp.zeros((1, width), jnp.float32)
    for q, v in reversed(levels[:-1]):
        n = q.shape[0]
        half = n // 2
        upper = m[:half]
        shift = jnp.concatenate([jnp.zeros((half, top.shape[1] - 1, width), jnp.float32), v[1 : 2 * half : 2, None, :]], axis=1)
        left = matmat(upper, q[1 : 2 * half : 2]) + shift
        m_new = jnp.stack([left, upper], axis=1).reshape((2 * half,) + upper.shape[1:])
        if n % 2:
            m_new = jnp.concatenate([m_new, m[-1:]], axis=0)
        m = m_new
    del offset_row
    return m


def place(b):
    inner = lax.axis_size("inner")
    return (b % inner) * lax.axis_size("outer") + b // inner


def exchange(x, d, count):
    return lax.ppermute(x, AXES, [(place(j), place(j ^ d)) for j in range(count)])


def body(propagator_matrices, smoothed_adjoints, station_loadings, offset_response):
    blocks = propagator_matrices[0]
    grads = smoothed_adjoints[0]
    width = grads.shape[1]
    stations = station_loadings.shape[3]
    count = lax.axis_size("outer") * lax.axis_size("inner")
    me = lax.axis_index("outer") * lax.axis_size("inner") + lax.axis_index("inner")

    leaf_v = vecmat(grads, blocks)
    levels = upsweep(blocks, leaf_v)
    tq, tv = levels[-1]
    tq, tv = tq[0].astype(jnp.float32), tv[0]
    sq = jnp.eye(width, dtype=jnp.float32)
    sv = jnp.zeros((width,), jnp.float32)

    d = 1
    while 2 * d < count:
        lower = (me // d) % 2 == 0
        got = exchange(jnp.concatenate([tq, tv[None, :]], axis=0), d, count)
        rq, rv = got[:width], got[width]
        q_up = jnp.where(lower, rq, tq)
        q_low = jnp.where(lower, tq, rq)
        v_up = jnp.where(lower, rv, tv)
        v_low = jnp.where(lower, tv, rv)
        both = jnp.dot(q_up, jnp.concatenate([q_low, sq], axis=1), precision=EXACT)
        new_sv = jnp.sum(rv[:, None] * sq, axis=0) + sv
        tv = jnp.sum(v_up[:, None] * q_low, axis=0) + v_low
        tq = both[:, :width]
        sq = jnp.where(lower, both[:, width:], sq)
        sv = jnp.where(lower, new_sv, sv)
        d *= 2
    lower = (me // d) % 2 == 0
    rv = exchange(tv, d, count)
    incoming = jnp.where(lower, jnp.sum(rv[:, None] * sq, axis=0) + sv, sv)

    top = jnp.concatenate([jnp.eye(width, dtype=jnp.float32), jnp.zeros((1, width), jnp.float32)], axis=0)
    maps = downsweep(levels, top[None])
    after = jnp.sum(incoming[None, :, None] * maps[:, :width, :], axis=1) + maps[:, width, :]
    length_rates = grads + after
    argument_values = station_loadings[0]
    local_kernel = jnp.dot(
        length_rates[:, :stations].T, argument_values[:, 0, :], precision=EXACT
    )
    local_kernel = local_kernel + jnp.dot(
        length_rates[:, stations:].T, argument_values[:, 1, :], precision=EXACT
    )
    local_noise = -jnp.sum(length_rates * offset_response[0])
    noise_row = jnp.zeros((1, local_kernel.shape[1]), jnp.float32).at[0, 0].set(local_noise)
    packed = jnp.concatenate([local_kernel, noise_row], axis=0)
    d = 1
    while d < count:
        packed = packed + exchange(packed, d, count)
        d *= 2
    return (length_rates[None], packed[:stations], packed[stations, 0])


def solution(mesh):
    return jax.shard_map(
        body,
        mesh=mesh,
        in_specs=(
            P("outer", "inner", None, None),
            P("outer", "inner", None),
            P("outer", "inner", None, None),
            P("outer", "inner", None),
        ),
        out_specs=(P("outer", "inner", None), P(), P()),
        check_vma=False,
    )
```

```python
import jax
import jax.numpy as jnp
from jax import lax
from jax.sharding import PartitionSpec as P

EXACT = lax.Precision.HIGHEST
AXES = ("inner", "outer")


def vecmat(v, q):
    return jnp.sum(v[:, :, None] * q.astype(jnp.float32), axis=1)


def matmat(later, earlier):
    if later.dtype == jnp.bfloat16 and earlier.dtype == jnp.bfloat16:
        return jnp.einsum("nij,njk->nik", later, earlier, preferred_element_type=jnp.float32)
    return jnp.einsum(
        "nij,njk->nik", later.astype(jnp.float32), earlier.astype(jnp.float32), precision=EXACT
    )


def upsweep(q, v):
    levels = [(q, v)]
    while q.shape[0] > 1:
        n = q.shape[0]
        half = n // 2
        qa, qb = q[0 : 2 * half : 2], q[1 : 2 * half : 2]
        va, vb = v[0 : 2 * half : 2], v[1 : 2 * half : 2]
        nq = matmat(qb, qa)
        nv = vecmat(vb, qa) + va
        if n % 2:
            nq = jnp.concatenate([nq, q[-1:].astype(jnp.float32)], axis=0)
            nv = jnp.concatenate([nv, v[-1:]], axis=0)
        q, v = nq, nv
        levels.append((q, v))
    return levels


def downsweep(levels, incoming):
    m = incoming
    for q, v in reversed(levels[:-1]):
        n = q.shape[0]
        half = n // 2
        upper = m[:half]
        left = vecmat(upper, q[1 : 2 * half : 2]) + v[1 : 2 * half : 2]
        m_new = jnp.stack([left, upper], axis=1).reshape(2 * half, -1)
        if n % 2:
            m_new = jnp.concatenate([m_new, m[-1:]], axis=0)
        m = m_new
    return m


def place(b):
    inner = lax.axis_size("inner")
    return (b % inner) * lax.axis_size("outer") + b // inner


def exchange(x, mask, count):
    return lax.ppermute(x, AXES, [(place(j), place(j ^ mask)) for j in range(count)])


def body(propagator_matrices, smoothed_adjoints, station_loadings, offset_response):
    blocks = propagator_matrices[0]
    grads = smoothed_adjoints[0]
    width = grads.shape[1]
    stations = station_loadings.shape[3]
    count = lax.axis_size("outer") * lax.axis_size("inner")
    me = lax.axis_index("outer") * lax.axis_size("inner") + lax.axis_index("inner")

    leaf_v = vecmat(grads, blocks)
    levels = upsweep(blocks, leaf_v)
    tq, tv = levels[-1]
    tq, tv = tq[0].astype(jnp.float32), tv[0]
    sq = jnp.eye(width, dtype=jnp.float32)
    sv = jnp.zeros((width,), jnp.float32)

    d = 1
    while 2 * d < count:
        lower = (me // d) % 2 == 0
        got = exchange(jnp.concatenate([tq, tv[None, :]], axis=0), d, count)
        rq, rv = got[:width], got[width]
        q_up = jnp.where(lower, rq, tq)
        q_low = jnp.where(lower, tq, rq)
        v_up = jnp.where(lower, rv, tv)
        v_low = jnp.where(lower, tv, rv)
        both = jnp.dot(q_up, jnp.concatenate([q_low, sq], axis=1), precision=EXACT)
        new_sv = jnp.sum(rv[:, None] * sq, axis=0) + sv
        tv = jnp.sum(v_up[:, None] * q_low, axis=0) + v_low
        tq = both[:, :width]
        sq = jnp.where(lower, both[:, width:], sq)
        sv = jnp.where(lower, new_sv, sv)
        d *= 2
    lower = (me // d) % 2 == 0
    rv = exchange(tv, d, count)
    incoming = jnp.where(lower, jnp.sum(rv[:, None] * sq, axis=0) + sv, sv)

    after = downsweep(levels, incoming[None, :])
    length_rates = grads + after
    argument_values = station_loadings[0]
    local_kernel = jnp.dot(
        length_rates[:, :stations].T, argument_values[:, 0, :], precision=EXACT
    )
    local_kernel = local_kernel + jnp.dot(
        length_rates[:, stations:].T, argument_values[:, 1, :], precision=EXACT
    )
    local_noise = -jnp.sum(length_rates * offset_response[0])
    noise_row = jnp.zeros((1, local_kernel.shape[1]), jnp.float32).at[0, 0].set(local_noise)
    packed = jnp.concatenate([local_kernel, noise_row], axis=0)
    low = 1
    while low < count:
        high = min(low * 8, count)
        vals = [packed] + [exchange(packed, m, count) for m in range(low, high, low)]
        while len(vals) > 1:
            vals = [vals[i] + vals[i + 1] for i in range(0, len(vals), 2)]
        packed = vals[0]
        low = high
    return (length_rates[None], packed[:stations], packed[stations, 0])


def solution(mesh):
    return jax.shard_map(
        body,
        mesh=mesh,
        in_specs=(
            P("outer", "inner", None, None),
            P("outer", "inner", None),
            P("outer", "inner", None, None),
            P("outer", "inner", None),
        ),
        out_specs=(P("outer", "inner", None), P(), P()),
        check_vma=False,
    )
```

```python
import jax
import jax.numpy as jnp
from jax import lax
from jax.sharding import PartitionSpec as P

EXACT = lax.Precision.HIGHEST
AXES = ("inner", "outer")


def vecmat(v, q):
    return jnp.sum(v[:, :, None] * q.astype(jnp.float32), axis=1)


def matmat(later, earlier):
    if later.dtype == jnp.bfloat16 and earlier.dtype == jnp.bfloat16:
        return jnp.einsum("nij,njk->nik", later, earlier, preferred_element_type=jnp.float32)
    return jnp.einsum(
        "nij,njk->nik", later.astype(jnp.float32), earlier.astype(jnp.float32), precision=EXACT
    )


def upsweep(q, v):
    levels = [(q, v)]
    while q.shape[0] > 1:
        n = q.shape[0]
        half = n // 2
        qa, qb = q[0 : 2 * half : 2], q[1 : 2 * half : 2]
        va, vb = v[0 : 2 * half : 2], v[1 : 2 * half : 2]
        nq = matmat(qb, qa)
        nv = vecmat(vb, qa) + va
        if n % 2:
            nq = jnp.concatenate([nq, q[-1:].astype(jnp.float32)], axis=0)
            nv = jnp.concatenate([nv, v[-1:]], axis=0)
        q, v = nq, nv
        levels.append((q, v))
    return levels


def downsweep(levels, incoming):
    m = incoming
    for q, v in reversed(levels[:-1]):
        n = q.shape[0]
        half = n // 2
        upper = m[:half]
        left = vecmat(upper, q[1 : 2 * half : 2]) + v[1 : 2 * half : 2]
        m_new = jnp.stack([left, upper], axis=1).reshape(2 * half, -1)
        if n % 2:
            m_new = jnp.concatenate([m_new, m[-1:]], axis=0)
        m = m_new
    return m


def place(b):
    inner = lax.axis_size("inner")
    return (b % inner) * lax.axis_size("outer") + b // inner


def exchange(x, mask, count):
    return lax.ppermute(x, AXES, [(place(j), place(j ^ mask)) for j in range(count)])


def body(propagator_matrices, smoothed_adjoints, station_loadings, offset_response):
    blocks = propagator_matrices[0]
    grads = smoothed_adjoints[0]
    width = grads.shape[1]
    stations = station_loadings.shape[3]
    count = lax.axis_size("outer") * lax.axis_size("inner")
    me = lax.axis_index("outer") * lax.axis_size("inner") + lax.axis_index("inner")

    leaf_v = vecmat(grads, blocks)
    levels = upsweep(blocks, leaf_v)
    tq, tv = levels[-1]
    tq, tv = tq[0].astype(jnp.float32), tv[0]
    sq = jnp.eye(width, dtype=jnp.float32)
    sv = jnp.zeros((width,), jnp.float32)

    packed = jnp.concatenate([tq, tv[None, :]], axis=0)
    d = 1
    while 2 * d < count:
        lower = (me // d) % 2 == 0
        got = exchange(packed, d, count)
        later = jnp.where(lower, got, packed)
        earlier_q = jnp.where(lower, packed[:width], got[:width])
        earlier_v = jnp.where(lower, packed[width], got[width])
        both = jnp.dot(later, jnp.concatenate([earlier_q, sq], axis=1), precision=EXACT)
        offset = jnp.zeros((width + 1, width), jnp.float32).at[width].set(earlier_v)
        packed = both[:, :width] + offset
        sq = jnp.where(lower, both[:width, width:], sq)
        sv = jnp.where(lower, both[width, width:] + sv, sv)
        d *= 2
    lower = (me // d) % 2 == 0
    rv = exchange(packed[width], d, count)
    incoming = jnp.where(lower, jnp.sum(rv[:, None] * sq, axis=0) + sv, sv)

    after = downsweep(levels, incoming[None, :])
    length_rates = grads + after
    argument_values = station_loadings[0]
    local_kernel = jnp.dot(
        length_rates[:, :stations].T, argument_values[:, 0, :], precision=EXACT
    )
    local_kernel = local_kernel + jnp.dot(
        length_rates[:, stations:].T, argument_values[:, 1, :], precision=EXACT
    )
    local_noise = -jnp.sum(length_rates * offset_response[0])
    noise_row = jnp.zeros((1, local_kernel.shape[1]), jnp.float32).at[0, 0].set(local_noise)
    packed = jnp.concatenate([local_kernel, noise_row], axis=0)
    d = 1
    while d < count:
        packed = packed + exchange(packed, d, count)
        d *= 2
    return (length_rates[None], packed[:stations], packed[stations, 0])


def solution(mesh):
    return jax.shard_map(
        body,
        mesh=mesh,
        in_specs=(
            P("outer", "inner", None, None),
            P("outer", "inner", None),
            P("outer", "inner", None, None),
            P("outer", "inner", None),
        ),
        out_specs=(P("outer", "inner", None), P(), P()),
        check_vma=False,
    )
```

```python
import jax
import jax.numpy as jnp
from jax import lax
from jax.sharding import PartitionSpec as P

EXACT = lax.Precision.HIGHEST
AXES = ("inner", "outer")


def vecmat(v, q):
    return jnp.sum(v[:, :, None] * q.astype(jnp.float32), axis=1)


def vecmat_mxu(v, q):
    return jnp.einsum("nj,njk->nk", v, q.astype(jnp.float32), precision=EXACT)


def matmat(later, earlier):
    if later.dtype == jnp.bfloat16 and earlier.dtype == jnp.bfloat16:
        return jnp.einsum("nij,njk->nik", later, earlier, preferred_element_type=jnp.float32)
    return jnp.einsum(
        "nij,njk->nik", later.astype(jnp.float32), earlier.astype(jnp.float32), precision=EXACT
    )


def upsweep(q, v):
    levels = [(q, v)]
    while q.shape[0] > 1:
        n = q.shape[0]
        half = n // 2
        qa, qb = q[0 : 2 * half : 2], q[1 : 2 * half : 2]
        va, vb = v[0 : 2 * half : 2], v[1 : 2 * half : 2]
        nq = matmat(qb, qa)
        nv = vecmat(vb, qa) + va
        if n % 2:
            nq = jnp.concatenate([nq, q[-1:].astype(jnp.float32)], axis=0)
            nv = jnp.concatenate([nv, v[-1:]], axis=0)
        q, v = nq, nv
        levels.append((q, v))
    return levels


def downsweep(levels, incoming):
    m = incoming
    for q, v in reversed(levels[:-1]):
        n = q.shape[0]
        half = n // 2
        upper = m[:half]
        left = vecmat_mxu(upper, q[1 : 2 * half : 2]) + v[1 : 2 * half : 2]
        m_new = jnp.stack([left, upper], axis=1).reshape(2 * half, -1)
        if n % 2:
            m_new = jnp.concatenate([m_new, m[-1:]], axis=0)
        m = m_new
    return m


def place(b):
    inner = lax.axis_size("inner")
    return (b % inner) * lax.axis_size("outer") + b // inner


def exchange(x, mask, count):
    return lax.ppermute(x, AXES, [(place(j), place(j ^ mask)) for j in range(count)])


def body(propagator_matrices, smoothed_adjoints, station_loadings, offset_response):
    blocks = propagator_matrices[0]
    grads = smoothed_adjoints[0]
    width = grads.shape[1]
    stations = station_loadings.shape[3]
    count = lax.axis_size("outer") * lax.axis_size("inner")
    me = lax.axis_index("outer") * lax.axis_size("inner") + lax.axis_index("inner")

    leaf_v = vecmat(grads, blocks)
    levels = upsweep(blocks, leaf_v)
    tq, tv = levels[-1]
    tq, tv = tq[0].astype(jnp.float32), tv[0]
    sq = jnp.eye(width, dtype=jnp.float32)
    sv = jnp.zeros((width,), jnp.float32)

    packed = jnp.concatenate([tq, tv[None, :]], axis=0)
    d = 1
    while 2 * d < count:
        got = exchange(packed, d, count)

        def as_lower(packed, got, sq, sv):
            both = jnp.dot(got, jnp.concatenate([packed[:width], sq], axis=1), precision=EXACT)
            offset = jnp.zeros((width + 1, width), jnp.float32).at[width].set(packed[width])
            return both[:, :width] + offset, both[:width, width:], both[width, width:] + sv

        def as_upper(packed, got, sq, sv):
            new = jnp.dot(packed, got[:width], precision=EXACT)
            offset = jnp.zeros((width + 1, width), jnp.float32).at[width].set(got[width])
            return new + offset, sq, sv

        packed, sq, sv = lax.cond((me // d) % 2 == 0, as_lower, as_upper, packed, got, sq, sv)
        d *= 2
    lower = (me // d) % 2 == 0
    rv = exchange(packed[width], d, count)
    incoming = jnp.where(lower, jnp.sum(rv[:, None] * sq, axis=0) + sv, sv)

    after = downsweep(levels, incoming[None, :])
    length_rates = grads + after
    argument_values = station_loadings[0]
    local_kernel = jnp.dot(
        length_rates[:, :stations].T, argument_values[:, 0, :], precision=EXACT
    )
    local_kernel = local_kernel + jnp.dot(
        length_rates[:, stations:].T, argument_values[:, 1, :], precision=EXACT
    )
    local_noise = -jnp.sum(length_rates * offset_response[0])
    noise_row = jnp.zeros((1, local_kernel.shape[1]), jnp.float32).at[0, 0].set(local_noise)
    packed = jnp.concatenate([local_kernel, noise_row], axis=0)
    d = 1
    while d < count:
        packed = packed + exchange(packed, d, count)
        d *= 2
    return (length_rates[None], packed[:stations], packed[stations, 0])


def solution(mesh):
    return jax.shard_map(
        body,
        mesh=mesh,
        in_specs=(
            P("outer", "inner", None, None),
            P("outer", "inner", None),
            P("outer", "inner", None, None),
            P("outer", "inner", None),
        ),
        out_specs=(P("outer", "inner", None), P(), P()),
        check_vma=False,
    )
```

```python
import jax
import jax.numpy as jnp
from jax import lax
from jax.sharding import PartitionSpec as P

EXACT = lax.Precision.HIGHEST
AXES = ("inner", "outer")


def vecmat(v, q):
    return jnp.sum(v[:, :, None] * q.astype(jnp.float32), axis=1)


def vecmat_mxu(v, q):
    return jnp.einsum("nj,njk->nk", v, q.astype(jnp.float32), precision=EXACT)


def matmat(later, earlier):
    if later.dtype == jnp.bfloat16 and earlier.dtype == jnp.bfloat16:
        return jnp.einsum("nij,njk->nik", later, earlier, preferred_element_type=jnp.float32)
    return jnp.einsum(
        "nij,njk->nik", later.astype(jnp.float32), earlier.astype(jnp.float32), precision=EXACT
    )


def upsweep(q, v):
    levels = [(q, v)]
    while q.shape[0] > 1:
        n = q.shape[0]
        half = n // 2
        qa, qb = q[0 : 2 * half : 2], q[1 : 2 * half : 2]
        va, vb = v[0 : 2 * half : 2], v[1 : 2 * half : 2]
        nq = matmat(qb, qa)
        nv = vecmat(vb, qa) + va
        if n % 2:
            nq = jnp.concatenate([nq, q[-1:].astype(jnp.float32)], axis=0)
            nv = jnp.concatenate([nv, v[-1:]], axis=0)
        q, v = nq, nv
        levels.append((q, v))
    return levels


def downsweep(levels, incoming):
    m = incoming
    for q, v in reversed(levels[:-1]):
        n = q.shape[0]
        half = n // 2
        upper = m[:half]
        left = vecmat_mxu(upper, q[1 : 2 * half : 2]) + v[1 : 2 * half : 2]
        m_new = jnp.stack([left, upper], axis=1).reshape(2 * half, -1)
        if n % 2:
            m_new = jnp.concatenate([m_new, m[-1:]], axis=0)
        m = m_new
    return m


def place(b):
    inner = lax.axis_size("inner")
    return (b % inner) * lax.axis_size("outer") + b // inner


def exchange(x, mask, count):
    return lax.ppermute(x, AXES, [(place(j), place(j ^ mask)) for j in range(count)])


def body(propagator_matrices, smoothed_adjoints, station_loadings, offset_response):
    blocks = propagator_matrices[0]
    grads = smoothed_adjoints[0]
    width = grads.shape[1]
    stations = station_loadings.shape[3]
    count = lax.axis_size("outer") * lax.axis_size("inner")
    me = lax.axis_index("outer") * lax.axis_size("inner") + lax.axis_index("inner")

    leaf_v = vecmat(grads, blocks)
    levels = upsweep(blocks, leaf_v)
    tq, tv = levels[-1]
    tq, tv = tq[0].astype(jnp.float32), tv[0]
    sq = jnp.eye(width, dtype=jnp.float32)
    sv = jnp.zeros((width,), jnp.float32)

    packed = jnp.concatenate([tq, tv[None, :]], axis=0)
    d = 1
    while 2 * d < count:
        lower = (me // d) % 2 == 0
        got = exchange(packed, d, count)
        later = jnp.where(lower, got, packed)
        earlier_q = jnp.where(lower, packed[:width], got[:width])
        earlier_v = jnp.where(lower, packed[width], got[width])
        both = jnp.dot(later, jnp.concatenate([earlier_q, sq], axis=1), precision=EXACT)
        offset = jnp.zeros((width + 1, width), jnp.float32).at[width].set(earlier_v)
        packed = both[:, :width] + offset
        sq = jnp.where(lower, both[:width, width:], sq)
        sv = jnp.where(lower, both[width, width:] + sv, sv)
        d *= 2
    lower = (me // d) % 2 == 0
    rv = exchange(packed[width], d, count)
    incoming = jnp.where(lower, jnp.sum(rv[:, None] * sq, axis=0) + sv, sv)

    after = downsweep(levels, incoming[None, :])
    length_rates = grads + after
    argument_values = station_loadings[0]
    local_kernel = jnp.dot(
        length_rates[:, :stations].T, argument_values[:, 0, :], precision=EXACT
    )
    local_kernel = local_kernel + jnp.dot(
        length_rates[:, stations:].T, argument_values[:, 1, :], precision=EXACT
    )
    local_noise = -jnp.sum(length_rates * offset_response[0])
    noise_row = jnp.zeros((1, local_kernel.shape[1]), jnp.float32).at[0, 0].set(local_noise)
    packed = jnp.concatenate([local_kernel, noise_row], axis=0)
    d = 1
    while d < count:
        packed = packed + exchange(packed, d, count)
        d *= 2
    return (length_rates[None], packed[:stations], packed[stations, 0])


def solution(mesh):
    return jax.shard_map(
        body,
        mesh=mesh,
        in_specs=(
            P("outer", "inner", None, None),
            P("outer", "inner", None),
            P("outer", "inner", None, None),
            P("outer", "inner", None),
        ),
        out_specs=(P("outer", "inner", None), P(), P()),
        check_vma=False,
    )
```

```python
import jax
import jax.numpy as jnp
from jax import lax
from jax.experimental import pallas as pl
from jax.sharding import PartitionSpec as P

EXACT = lax.Precision.HIGHEST
AXES = ("inner", "outer")


def vecmat(v, q):
    return jnp.sum(v[:, :, None] * q.astype(jnp.float32), axis=1)


def vecmat_mxu(v, q):
    return jnp.einsum("nj,njk->nk", v, q.astype(jnp.float32), precision=EXACT)


def matmat(later, earlier):
    if later.dtype == jnp.bfloat16 and earlier.dtype == jnp.bfloat16:
        return jnp.einsum("nij,njk->nik", later, earlier, preferred_element_type=jnp.float32)
    return jnp.einsum(
        "nij,njk->nik", later.astype(jnp.float32), earlier.astype(jnp.float32), precision=EXACT
    )


def upsweep(q, v):
    levels = [(q, v)]
    while q.shape[0] > 1:
        n = q.shape[0]
        half = n // 2
        qa, qb = q[0 : 2 * half : 2], q[1 : 2 * half : 2]
        va, vb = v[0 : 2 * half : 2], v[1 : 2 * half : 2]
        nq = matmat(qb, qa)
        nv = vecmat(vb, qa) + va
        if n % 2:
            nq = jnp.concatenate([nq, q[-1:].astype(jnp.float32)], axis=0)
            nv = jnp.concatenate([nv, v[-1:]], axis=0)
        q, v = nq, nv
        levels.append((q, v))
    return levels


def downsweep(levels, incoming):
    m = incoming
    for q, v in reversed(levels[:-1]):
        n = q.shape[0]
        half = n // 2
        upper = m[:half]
        left = vecmat_mxu(upper, q[1 : 2 * half : 2]) + v[1 : 2 * half : 2]
        m_new = jnp.stack([left, upper], axis=1).reshape(2 * half, -1)
        if n % 2:
            m_new = jnp.concatenate([m_new, m[-1:]], axis=0)
        m = m_new
    return m


def scan_round(d, width):
    def kernel(own_ref, got_ref, sq_ref, sv_ref, own_out, sq_out, sv_out):
        me = lax.axis_index("outer") * lax.axis_size("inner") + lax.axis_index("inner")
        lower = (me // d) % 2 == 0
        later = jnp.where(lower, got_ref[...], own_ref[...])
        early_q = jnp.where(lower, own_ref[0:width, :], got_ref[0:width, :])
        early_v = jnp.where(lower, own_ref[width:, :], got_ref[width:, :])
        new_q = jnp.dot(later, early_q, precision=EXACT, preferred_element_type=jnp.float32)
        new_s = jnp.dot(later, sq_ref[...], precision=EXACT, preferred_element_type=jnp.float32)
        own_out[0:width, :] = new_q[0:width]
        own_out[width:, :] = new_q[width:] + early_v
        sq_out[...] = jnp.where(lower, new_s[0:width], sq_ref[...])
        sv_out[...] = jnp.where(lower, new_s[width:] + sv_ref[...], sv_ref[...])

    def run(own, got, sq, sv):
        return pl.pallas_call(
            kernel,
            out_shape=(
                jax.ShapeDtypeStruct(own.shape, jnp.float32),
                jax.ShapeDtypeStruct(sq.shape, jnp.float32),
                jax.ShapeDtypeStruct(sv.shape, jnp.float32),
            ),
        )(own, got, sq, sv)

    return run


def place(b):
    inner = lax.axis_size("inner")
    return (b % inner) * lax.axis_size("outer") + b // inner


def exchange(x, mask, count):
    return lax.ppermute(x, AXES, [(place(j), place(j ^ mask)) for j in range(count)])


def body(propagator_matrices, smoothed_adjoints, station_loadings, offset_response):
    blocks = propagator_matrices[0]
    grads = smoothed_adjoints[0]
    width = grads.shape[1]
    stations = station_loadings.shape[3]
    count = lax.axis_size("outer") * lax.axis_size("inner")
    me = lax.axis_index("outer") * lax.axis_size("inner") + lax.axis_index("inner")

    leaf_v = vecmat(grads, blocks)
    levels = upsweep(blocks, leaf_v)
    tq, tv = levels[-1]
    tq, tv = tq[0].astype(jnp.float32), tv[0]
    sq = jnp.eye(width, dtype=jnp.float32)
    sv = jnp.zeros((width,), jnp.float32)

    packed = jnp.concatenate([tq, tv[None, :], jnp.zeros((7, width), jnp.float32)], axis=0)
    sv = jnp.zeros((8, width), jnp.float32)
    d = 1
    while 2 * d < count:
        got = exchange(packed, d, count)
        packed, sq, sv = scan_round(d, width)(packed, got, sq, sv)
        d *= 2
    lower = (me // d) % 2 == 0
    rv = exchange(packed[width], d, count)
    incoming = jnp.where(lower, jnp.sum(rv[:, None] * sq, axis=0) + sv[0], sv[0])

    after = downsweep(levels, incoming[None, :])
    length_rates = grads + after
    argument_values = station_loadings[0]
    local_kernel = jnp.dot(
        length_rates[:, :stations].T, argument_values[:, 0, :], precision=EXACT
    )
    local_kernel = local_kernel + jnp.dot(
        length_rates[:, stations:].T, argument_values[:, 1, :], precision=EXACT
    )
    local_noise = -jnp.sum(length_rates * offset_response[0])
    noise_row = jnp.zeros((1, local_kernel.shape[1]), jnp.float32).at[0, 0].set(local_noise)
    packed = jnp.concatenate([local_kernel, noise_row], axis=0)
    d = 1
    while d < count:
        packed = packed + exchange(packed, d, count)
        d *= 2
    return (length_rates[None], packed[:stations], packed[stations, 0])


def solution(mesh):
    return jax.shard_map(
        body,
        mesh=mesh,
        in_specs=(
            P("outer", "inner", None, None),
            P("outer", "inner", None),
            P("outer", "inner", None, None),
            P("outer", "inner", None),
        ),
        out_specs=(P("outer", "inner", None), P(), P()),
        check_vma=False,
    )
```

```python
import jax
import jax.numpy as jnp
from jax import lax
from jax.experimental import pallas as pl
from jax.sharding import PartitionSpec as P

EXACT = lax.Precision.HIGHEST
AXES = ("inner", "outer")


def vecmat(v, q):
    return jnp.sum(v[:, :, None] * q.astype(jnp.float32), axis=1)


def vecmat_mxu(v, q):
    return jnp.einsum("nj,njk->nk", v, q.astype(jnp.float32), precision=EXACT)


def matmat(later, earlier):
    if later.dtype == jnp.bfloat16 and earlier.dtype == jnp.bfloat16:
        return jnp.einsum("nij,njk->nik", later, earlier, preferred_element_type=jnp.float32)
    return jnp.einsum(
        "nij,njk->nik", later.astype(jnp.float32), earlier.astype(jnp.float32), precision=EXACT
    )


def upsweep(q, v):
    levels = [(q, v)]
    while q.shape[0] > 1:
        n = q.shape[0]
        half = n // 2
        qa, qb = q[0 : 2 * half : 2], q[1 : 2 * half : 2]
        va, vb = v[0 : 2 * half : 2], v[1 : 2 * half : 2]
        nq = matmat(qb, qa)
        nv = vecmat(vb, qa) + va
        if n % 2:
            nq = jnp.concatenate([nq, q[-1:].astype(jnp.float32)], axis=0)
            nv = jnp.concatenate([nv, v[-1:]], axis=0)
        q, v = nq, nv
        levels.append((q, v))
    return levels


def downsweep(levels, incoming):
    m = incoming
    for q, v in reversed(levels[:-1]):
        n = q.shape[0]
        half = n // 2
        upper = m[:half]
        left = vecmat_mxu(upper, q[1 : 2 * half : 2]) + v[1 : 2 * half : 2]
        m_new = jnp.stack([left, upper], axis=1).reshape(2 * half, -1)
        if n % 2:
            m_new = jnp.concatenate([m_new, m[-1:]], axis=0)
        m = m_new
    return m


def scan_round(d, width):
    def kernel(own_ref, got_ref, sq_ref, sv_ref, own_out, sq_out, sv_out):
        me = lax.axis_index("outer") * lax.axis_size("inner") + lax.axis_index("inner")
        lower = (me // d) % 2 == 0
        later = jnp.where(lower, got_ref[...], own_ref[...])
        early_q = jnp.where(lower, own_ref[0:width, :], got_ref[0:width, :])
        early_v = jnp.where(lower, own_ref[width:, :], got_ref[width:, :])
        new_q = jnp.dot(later, early_q, precision=EXACT, preferred_element_type=jnp.float32)
        new_s = jnp.dot(later, sq_ref[...], precision=EXACT, preferred_element_type=jnp.float32)
        own_out[0:width, :] = new_q[0:width]
        own_out[width:, :] = new_q[width:] + early_v
        sq_out[...] = jnp.where(lower, new_s[0:width], sq_ref[...])
        sv_out[...] = jnp.where(lower, new_s[width:] + sv_ref[...], sv_ref[...])

    def run(own, got, sq, sv):
        return pl.pallas_call(
            kernel,
            out_shape=(
                jax.ShapeDtypeStruct(own.shape, jnp.float32),
                jax.ShapeDtypeStruct(sq.shape, jnp.float32),
                jax.ShapeDtypeStruct(sv.shape, jnp.float32),
            ),
        )(own, got, sq, sv)

    return run


def column(row):
    return jnp.broadcast_to(row, (8, row.shape[1])).T[:, 0:1]


def row_times(row, q):
    return jnp.sum(column(row) * q.astype(jnp.float32), axis=0, keepdims=True)


def finish(d, sizes, width):
    depth = len(sizes) - 1

    def kernel(*refs):
        rv_ref, sq_ref, sv_ref, grads_ref = refs[:4]
        tree = refs[4 : 4 + 2 * depth]
        out_ref = refs[4 + 2 * depth]
        me = lax.axis_index("outer") * lax.axis_size("inner") + lax.axis_index("inner")
        lower = (me // d) % 2 == 0
        sv = sv_ref[0:1, :]
        entering = jnp.where(lower, row_times(rv_ref[0:1, :], sq_ref[...]) + sv, sv)
        rows = [entering]
        for level in reversed(range(depth)):
            q_ref, v_ref = tree[2 * level], tree[2 * level + 1]
            n = sizes[level]
            new = []
            for j in range(n // 2):
                upper = rows[j]
                new.append(row_times(upper, q_ref[j]) + v_ref[j : j + 1, :])
                new.append(upper)
            if n % 2:
                new.append(rows[-1])
            rows = new
        for t, row in enumerate(rows):
            out_ref[t : t + 1, :] = grads_ref[t : t + 1, :] + row

    def run(rv, sq, sv, grads, levels):
        args = [rv, sq, sv, grads]
        for level in range(depth):
            q, v = levels[level]
            half = sizes[level] // 2
            args += [q[1 : 2 * half : 2], v[1 : 2 * half : 2]]
        return pl.pallas_call(
            kernel, out_shape=jax.ShapeDtypeStruct(grads.shape, jnp.float32)
        )(*args)

    return run


def place(b):
    inner = lax.axis_size("inner")
    return (b % inner) * lax.axis_size("outer") + b // inner


def exchange(x, mask, count):
    return lax.ppermute(x, AXES, [(place(j), place(j ^ mask)) for j in range(count)])


def body(propagator_matrices, smoothed_adjoints, station_loadings, offset_response):
    blocks = propagator_matrices[0]
    grads = smoothed_adjoints[0]
    width = grads.shape[1]
    stations = station_loadings.shape[3]
    count = lax.axis_size("outer") * lax.axis_size("inner")
    me = lax.axis_index("outer") * lax.axis_size("inner") + lax.axis_index("inner")

    leaf_v = vecmat(grads, blocks)
    levels = upsweep(blocks, leaf_v)
    tq, tv = levels[-1]
    tq, tv = tq[0].astype(jnp.float32), tv[0]
    sq = jnp.eye(width, dtype=jnp.float32)
    sv = jnp.zeros((width,), jnp.float32)

    packed = jnp.concatenate([tq, tv[None, :], jnp.zeros((7, width), jnp.float32)], axis=0)
    sv = jnp.zeros((8, width), jnp.float32)
    d = 1
    while 2 * d < count:
        got = exchange(packed, d, count)
        packed, sq, sv = scan_round(d, width)(packed, got, sq, sv)
        d *= 2
    rv = exchange(packed[width:], d, count)
    sizes = [level[0].shape[0] for level in levels]
    length_rates = finish(d, sizes, width)(rv, sq, sv, grads, levels)
    argument_values = station_loadings[0]
    local_kernel = jnp.dot(
        length_rates[:, :stations].T, argument_values[:, 0, :], precision=EXACT
    )
    local_kernel = local_kernel + jnp.dot(
        length_rates[:, stations:].T, argument_values[:, 1, :], precision=EXACT
    )
    local_noise = -jnp.sum(length_rates * offset_response[0])
    noise_row = jnp.zeros((1, local_kernel.shape[1]), jnp.float32).at[0, 0].set(local_noise)
    packed = jnp.concatenate([local_kernel, noise_row], axis=0)
    d = 1
    while d < count:
        packed = packed + exchange(packed, d, count)
        d *= 2
    return (length_rates[None], packed[:stations], packed[stations, 0])


def solution(mesh):
    return jax.shard_map(
        body,
        mesh=mesh,
        in_specs=(
            P("outer", "inner", None, None),
            P("outer", "inner", None),
            P("outer", "inner", None, None),
            P("outer", "inner", None),
        ),
        out_specs=(P("outer", "inner", None), P(), P()),
        check_vma=False,
    )
```

```python
import jax
import jax.numpy as jnp
from jax import lax
from jax.experimental import pallas as pl
from jax.sharding import PartitionSpec as P

EXACT = lax.Precision.HIGHEST
AXES = ("inner", "outer")


def vecmat(v, q):
    return jnp.sum(v[:, :, None] * q.astype(jnp.float32), axis=1)


def vecmat_mxu(v, q):
    return jnp.einsum("nj,njk->nk", v, q.astype(jnp.float32), precision=EXACT)


def matmat(later, earlier):
    if later.dtype == jnp.bfloat16 and earlier.dtype == jnp.bfloat16:
        return jnp.einsum("nij,njk->nik", later, earlier, preferred_element_type=jnp.float32)
    return jnp.einsum(
        "nij,njk->nik", later.astype(jnp.float32), earlier.astype(jnp.float32), precision=EXACT
    )


def upsweep(q, v):
    levels = [(q, v)]
    while q.shape[0] > 1:
        n = q.shape[0]
        half = n // 2
        qa, qb = q[0 : 2 * half : 2], q[1 : 2 * half : 2]
        va, vb = v[0 : 2 * half : 2], v[1 : 2 * half : 2]
        nq = matmat(qb, qa)
        nv = vecmat(vb, qa) + va
        if n % 2:
            nq = jnp.concatenate([nq, q[-1:].astype(jnp.float32)], axis=0)
            nv = jnp.concatenate([nv, v[-1:]], axis=0)
        q, v = nq, nv
        levels.append((q, v))
    return levels


def downsweep(levels, incoming):
    m = incoming
    for q, v in reversed(levels[:-1]):
        n = q.shape[0]
        half = n // 2
        upper = m[:half]
        left = vecmat_mxu(upper, q[1 : 2 * half : 2]) + v[1 : 2 * half : 2]
        m_new = jnp.stack([left, upper], axis=1).reshape(2 * half, -1)
        if n % 2:
            m_new = jnp.concatenate([m_new, m[-1:]], axis=0)
        m = m_new
    return m


def scan_round(d, width):
    def kernel(own_ref, got_ref, sq_ref, sv_ref, own_out, sq_out, sv_out):
        me = lax.axis_index("outer") * lax.axis_size("inner") + lax.axis_index("inner")
        lower = (me // d) % 2 == 0
        later = jnp.where(lower, got_ref[...], own_ref[...])
        early_q = jnp.where(lower, own_ref[0:width, :], got_ref[0:width, :])
        early_v = jnp.where(lower, own_ref[width:, :], got_ref[width:, :])
        new_q = jnp.dot(later, early_q, precision=EXACT, preferred_element_type=jnp.float32)
        new_s = jnp.dot(later, sq_ref[...], precision=EXACT, preferred_element_type=jnp.float32)
        own_out[0:width, :] = new_q[0:width]
        own_out[width:, :] = new_q[width:] + early_v
        sq_out[...] = jnp.where(lower, new_s[0:width], sq_ref[...])
        sv_out[...] = jnp.where(lower, new_s[width:] + sv_ref[...], sv_ref[...])

    def run(own, got, sq, sv):
        return pl.pallas_call(
            kernel,
            out_shape=(
                jax.ShapeDtypeStruct(own.shape, jnp.float32),
                jax.ShapeDtypeStruct(sq.shape, jnp.float32),
                jax.ShapeDtypeStruct(sv.shape, jnp.float32),
            ),
        )(own, got, sq, sv)

    return run


def column(row):
    return jnp.broadcast_to(row, (8, row.shape[1])).T[:, 0:1]


def row_times(row, q):
    return jnp.sum(column(row) * q.astype(jnp.float32), axis=0, keepdims=True)


def finish(d, sizes, width, stations):
    depth = len(sizes) - 1

    def kernel(*refs):
        rv_ref, sq_ref, sv_ref, grads_ref, load_ref, resp_ref = refs[:6]
        tree = refs[6 : 6 + 2 * depth]
        out_ref = refs[6 + 2 * depth]
        me = lax.axis_index("outer") * lax.axis_size("inner") + lax.axis_index("inner")
        lower = (me // d) % 2 == 0
        sv = sv_ref[0:1, :]
        entering = jnp.where(lower, row_times(rv_ref[0:1, :], sq_ref[...]) + sv, sv)
        rows = [entering]
        for level in reversed(range(depth)):
            q_ref, v_ref = tree[2 * level], tree[2 * level + 1]
            n = sizes[level]
            new = []
            for j in range(n // 2):
                upper = rows[j]
                new.append(row_times(upper, q_ref[2 * j + 1]) + v_ref[2 * j + 1 : 2 * j + 2, :])
                new.append(upper)
            if n % 2:
                new.append(rows[-1])
            rows = new
        for t, row in enumerate(rows):
            out_ref[t : t + 1, :] = grads_ref[t : t + 1, :] + row

    def run(rv, sq, sv, grads, loads, resp, levels):
        args = [rv, sq, sv, grads, loads, resp]
        for level in range(depth):
            args += list(levels[level])
        return pl.pallas_call(
            kernel,
            out_shape=jax.ShapeDtypeStruct(grads.shape, jnp.float32),
        )(*args)

    return run


def place(b):
    inner = lax.axis_size("inner")
    return (b % inner) * lax.axis_size("outer") + b // inner


def exchange(x, mask, count):
    return lax.ppermute(x, AXES, [(place(j), place(j ^ mask)) for j in range(count)])


def body(propagator_matrices, smoothed_adjoints, station_loadings, offset_response):
    blocks = propagator_matrices[0]
    grads = smoothed_adjoints[0]
    width = grads.shape[1]
    stations = station_loadings.shape[3]
    count = lax.axis_size("outer") * lax.axis_size("inner")
    me = lax.axis_index("outer") * lax.axis_size("inner") + lax.axis_index("inner")

    leaf_v = vecmat(grads, blocks)
    levels = upsweep(blocks, leaf_v)
    tq, tv = levels[-1]
    tq, tv = tq[0].astype(jnp.float32), tv[0]
    sq = jnp.eye(width, dtype=jnp.float32)
    sv = jnp.zeros((width,), jnp.float32)

    packed = jnp.concatenate([tq, tv[None, :], jnp.zeros((7, width), jnp.float32)], axis=0)
    sv = jnp.zeros((8, width), jnp.float32)
    d = 1
    while 2 * d < count:
        got = exchange(packed, d, count)
        packed, sq, sv = scan_round(d, width)(packed, got, sq, sv)
        d *= 2
    rv = exchange(packed[width:], d, count)
    sizes = [level[0].shape[0] for level in levels]
    length_rates = finish(d, sizes, width, stations)(
        rv, sq, sv, grads, station_loadings[0], offset_response[0], levels
    )
    argument_values = station_loadings[0]
    local_kernel = jnp.dot(
        length_rates[:, :stations].T, argument_values[:, 0, :], precision=EXACT
    )
    local_kernel = local_kernel + jnp.dot(
        length_rates[:, stations:].T, argument_values[:, 1, :], precision=EXACT
    )
    local_noise = -jnp.sum(length_rates * offset_response[0])
    noise_row = jnp.zeros((1, local_kernel.shape[1]), jnp.float32).at[0, 0].set(local_noise)
    packed = jnp.concatenate([local_kernel, noise_row], axis=0)
    d = 1
    while d < count:
        packed = packed + exchange(packed, d, count)
        d *= 2
    return (length_rates[None], packed[:stations], packed[stations, 0])


def solution(mesh):
    return jax.shard_map(
        body,
        mesh=mesh,
        in_specs=(
            P("outer", "inner", None, None),
            P("outer", "inner", None),
            P("outer", "inner", None, None),
            P("outer", "inner", None),
        ),
        out_specs=(P("outer", "inner", None), P(), P()),
        check_vma=False,
    )
```

```python
import jax
import jax.numpy as jnp
from jax import lax
from jax.experimental import pallas as pl
from jax.sharding import PartitionSpec as P

EXACT = lax.Precision.HIGHEST
AXES = ("inner", "outer")


def vecmat(v, q):
    return jnp.sum(v[:, :, None] * q.astype(jnp.float32), axis=1)


def vecmat_mxu(v, q):
    return jnp.einsum("nj,njk->nk", v, q.astype(jnp.float32), precision=EXACT)


def matmat(later, earlier):
    if later.dtype == jnp.bfloat16 and earlier.dtype == jnp.bfloat16:
        return jnp.einsum("nij,njk->nik", later, earlier, preferred_element_type=jnp.float32)
    return jnp.einsum(
        "nij,njk->nik", later.astype(jnp.float32), earlier.astype(jnp.float32), precision=EXACT
    )


def upsweep(q, v):
    levels = [(q, v)]
    while q.shape[0] > 1:
        n = q.shape[0]
        half = n // 2
        qa, qb = q[0 : 2 * half : 2], q[1 : 2 * half : 2]
        va, vb = v[0 : 2 * half : 2], v[1 : 2 * half : 2]
        nq = matmat(qb, qa)
        nv = vecmat(vb, qa) + va
        if n % 2:
            nq = jnp.concatenate([nq, q[-1:].astype(jnp.float32)], axis=0)
            nv = jnp.concatenate([nv, v[-1:]], axis=0)
        q, v = nq, nv
        levels.append((q, v))
    return levels


def downsweep(levels, incoming):
    m = incoming
    for q, v in reversed(levels[:-1]):
        n = q.shape[0]
        half = n // 2
        upper = m[:half]
        left = vecmat_mxu(upper, q[1 : 2 * half : 2]) + v[1 : 2 * half : 2]
        m_new = jnp.stack([left, upper], axis=1).reshape(2 * half, -1)
        if n % 2:
            m_new = jnp.concatenate([m_new, m[-1:]], axis=0)
        m = m_new
    return m


def scan_round(d, width):
    def lower_half():
        me = lax.axis_index("outer") * lax.axis_size("inner") + lax.axis_index("inner")
        return (me // d) % 2 == 0

    def group_kernel(own_ref, got_ref, own_out):
        lower = lower_half()
        later = jnp.where(lower, got_ref[...], own_ref[...])
        early_q = jnp.where(lower, own_ref[0:width, :], got_ref[0:width, :])
        early_v = jnp.where(lower, own_ref[width:, :], got_ref[width:, :])
        new_q = jnp.dot(later, early_q, precision=EXACT, preferred_element_type=jnp.float32)
        own_out[0:width, :] = new_q[0:width]
        own_out[width:, :] = new_q[width:] + early_v

    def suffix_kernel(got_ref, sq_ref, sv_ref, sq_out, sv_out):
        lower = lower_half()
        new_s = jnp.dot(got_ref[...], sq_ref[...], precision=EXACT, preferred_element_type=jnp.float32)
        sq_out[...] = jnp.where(lower, new_s[0:width], sq_ref[...])
        sv_out[...] = jnp.where(lower, new_s[width:] + sv_ref[...], sv_ref[...])

    def run(own, got, sq, sv):
        new = pl.pallas_call(group_kernel, out_shape=jax.ShapeDtypeStruct(own.shape, jnp.float32))(own, got)
        sq, sv = pl.pallas_call(
            suffix_kernel,
            out_shape=(
                jax.ShapeDtypeStruct(sq.shape, jnp.float32),
                jax.ShapeDtypeStruct(sv.shape, jnp.float32),
            ),
        )(got, sq, sv)
        return new, sq, sv

    return run


def column(row):
    return jnp.broadcast_to(row, (8, row.shape[1])).T[:, 0:1]


def row_times(row, q):
    return jnp.sum(column(row) * q.astype(jnp.float32), axis=0, keepdims=True)


def finish(d, sizes, width, stations):
    depth = len(sizes) - 1

    def kernel(*refs):
        rv_ref, sq_ref, sv_ref, grads_ref, load_ref, resp_ref = refs[:6]
        tree = refs[6 : 6 + 2 * depth]
        out_ref = refs[6 + 2 * depth]
        me = lax.axis_index("outer") * lax.axis_size("inner") + lax.axis_index("inner")
        lower = (me // d) % 2 == 0
        sv = sv_ref[0:1, :]
        entering = jnp.where(lower, row_times(rv_ref[0:1, :], sq_ref[...]) + sv, sv)
        rows = [entering]
        for level in reversed(range(depth)):
            q_ref, v_ref = tree[2 * level], tree[2 * level + 1]
            n = sizes[level]
            new = []
            for j in range(n // 2):
                upper = rows[j]
                new.append(row_times(upper, q_ref[2 * j + 1]) + v_ref[2 * j + 1 : 2 * j + 2, :])
                new.append(upper)
            if n % 2:
                new.append(rows[-1])
            rows = new
        for t, row in enumerate(rows):
            out_ref[t : t + 1, :] = grads_ref[t : t + 1, :] + row

    def run(rv, sq, sv, grads, loads, resp, levels):
        args = [rv, sq, sv, grads, loads, resp]
        for level in range(depth):
            args += list(levels[level])
        return pl.pallas_call(
            kernel,
            out_shape=jax.ShapeDtypeStruct(grads.shape, jnp.float32),
        )(*args)

    return run


def place(b):
    inner = lax.axis_size("inner")
    return (b % inner) * lax.axis_size("outer") + b // inner


def exchange(x, mask, count):
    return lax.ppermute(x, AXES, [(place(j), place(j ^ mask)) for j in range(count)])


def body(propagator_matrices, smoothed_adjoints, station_loadings, offset_response):
    blocks = propagator_matrices[0]
    grads = smoothed_adjoints[0]
    width = grads.shape[1]
    stations = station_loadings.shape[3]
    count = lax.axis_size("outer") * lax.axis_size("inner")
    me = lax.axis_index("outer") * lax.axis_size("inner") + lax.axis_index("inner")

    leaf_v = vecmat(grads, blocks)
    levels = upsweep(blocks, leaf_v)
    tq, tv = levels[-1]
    tq, tv = tq[0].astype(jnp.float32), tv[0]
    sq = jnp.eye(width, dtype=jnp.float32)
    sv = jnp.zeros((width,), jnp.float32)

    packed = jnp.concatenate([tq, tv[None, :], jnp.zeros((7, width), jnp.float32)], axis=0)
    sv = jnp.zeros((8, width), jnp.float32)
    d = 1
    while 2 * d < count:
        got = exchange(packed, d, count)
        packed, sq, sv = scan_round(d, width)(packed, got, sq, sv)
        d *= 2
    rv = exchange(packed[width:], d, count)
    sizes = [level[0].shape[0] for level in levels]
    length_rates = finish(d, sizes, width, stations)(
        rv, sq, sv, grads, station_loadings[0], offset_response[0], levels
    )
    argument_values = station_loadings[0]
    local_kernel = jnp.dot(
        length_rates[:, :stations].T, argument_values[:, 0, :], precision=EXACT
    )
    local_kernel = local_kernel + jnp.dot(
        length_rates[:, stations:].T, argument_values[:, 1, :], precision=EXACT
    )
    local_noise = -jnp.sum(length_rates * offset_response[0])
    noise_row = jnp.zeros((1, local_kernel.shape[1]), jnp.float32).at[0, 0].set(local_noise)
    packed = jnp.concatenate([local_kernel, noise_row], axis=0)
    d = 1
    while d < count:
        packed = packed + exchange(packed, d, count)
        d *= 2
    return (length_rates[None], packed[:stations], packed[stations, 0])


def solution(mesh):
    return jax.shard_map(
        body,
        mesh=mesh,
        in_specs=(
            P("outer", "inner", None, None),
            P("outer", "inner", None),
            P("outer", "inner", None, None),
            P("outer", "inner", None),
        ),
        out_specs=(P("outer", "inner", None), P(), P()),
        check_vma=False,
    )
```

```python
import jax
import jax.numpy as jnp
from jax import lax
from jax.experimental import pallas as pl
from jax.sharding import PartitionSpec as P

EXACT = lax.Precision.HIGHEST
AXES = ("inner", "outer")


def vecmat(v, q):
    return jnp.sum(v[:, :, None] * q.astype(jnp.float32), axis=1)


def vecmat_mxu(v, q):
    return jnp.einsum("nj,njk->nk", v, q.astype(jnp.float32), precision=EXACT)


def matmat(later, earlier):
    if later.dtype == jnp.bfloat16 and earlier.dtype == jnp.bfloat16:
        return jnp.einsum("nij,njk->nik", later, earlier, preferred_element_type=jnp.float32)
    return jnp.einsum(
        "nij,njk->nik", later.astype(jnp.float32), earlier.astype(jnp.float32), precision=EXACT
    )


def upsweep(q, v):
    levels = [(q, v)]
    while q.shape[0] > 1:
        n = q.shape[0]
        half = n // 2
        qa, qb = q[0 : 2 * half : 2], q[1 : 2 * half : 2]
        va, vb = v[0 : 2 * half : 2], v[1 : 2 * half : 2]
        nq = matmat(qb, qa)
        nv = vecmat(vb, qa) + va
        if n % 2:
            nq = jnp.concatenate([nq, q[-1:].astype(jnp.float32)], axis=0)
            nv = jnp.concatenate([nv, v[-1:]], axis=0)
        q, v = nq, nv
        levels.append((q, v))
    return levels


def downsweep(levels, incoming):
    m = incoming
    for q, v in reversed(levels[:-1]):
        n = q.shape[0]
        half = n // 2
        upper = m[:half]
        left = vecmat_mxu(upper, q[1 : 2 * half : 2]) + v[1 : 2 * half : 2]
        m_new = jnp.stack([left, upper], axis=1).reshape(2 * half, -1)
        if n % 2:
            m_new = jnp.concatenate([m_new, m[-1:]], axis=0)
        m = m_new
    return m


def scan_round(d, width):
    def kernel(own_ref, got_ref, sq_ref, sv_ref, own_out, sq_out, sv_out):
        me = lax.axis_index("outer") * lax.axis_size("inner") + lax.axis_index("inner")
        lower = (me // d) % 2 == 0
        later = jnp.where(lower, got_ref[...], own_ref[...])
        early_q = jnp.where(lower, own_ref[0:width, :], got_ref[0:width, :])
        early_v = jnp.where(lower, own_ref[width:, :], got_ref[width:, :])
        new_q = jnp.dot(later, early_q, precision=EXACT, preferred_element_type=jnp.float32)
        new_s = jnp.dot(later, sq_ref[...], precision=EXACT, preferred_element_type=jnp.float32)
        own_out[0:width, :] = new_q[0:width]
        own_out[width:, :] = new_q[width:] + early_v
        sq_out[...] = jnp.where(lower, new_s[0:width], sq_ref[...])
        sv_out[...] = jnp.where(lower, new_s[width:] + sv_ref[...], sv_ref[...])

    def run(own, got, sq, sv):
        return pl.pallas_call(
            kernel,
            out_shape=(
                jax.ShapeDtypeStruct(own.shape, jnp.float32),
                jax.ShapeDtypeStruct(sq.shape, jnp.float32),
                jax.ShapeDtypeStruct(sv.shape, jnp.float32),
            ),
        )(own, got, sq, sv)

    return run


def column(row):
    return jnp.broadcast_to(row, (8, row.shape[1])).T[:, 0:1]


def row_times(row, q):
    return jnp.sum(column(row) * q.astype(jnp.float32), axis=0, keepdims=True)


def finish(d, sizes, width, stations):
    depth = len(sizes) - 1

    def kernel(*refs):
        rv_ref, sq_ref, sv_ref, grads_ref, load_ref, resp_ref = refs[:6]
        tree = refs[6 : 6 + 2 * depth]
        out_ref, grad_ref = refs[6 + 2 * depth :]
        me = lax.axis_index("outer") * lax.axis_size("inner") + lax.axis_index("inner")
        lower = (me // d) % 2 == 0
        sv = sv_ref[0:1, :]
        entering = jnp.where(lower, row_times(rv_ref[0:1, :], sq_ref[...]) + sv, sv)
        rows = [entering]
        for level in reversed(range(depth)):
            q_ref, v_ref = tree[2 * level], tree[2 * level + 1]
            n = sizes[level]
            new = []
            for j in range(n // 2):
                upper = rows[j]
                new.append(row_times(upper, q_ref[2 * j + 1]) + v_ref[2 * j + 1 : 2 * j + 2, :])
                new.append(upper)
            if n % 2:
                new.append(rows[-1])
            rows = new
        kernel_grad = jnp.zeros((stations, stations), jnp.float32)
        for t, row in enumerate(rows):
            rate = grads_ref[t : t + 1, :] + row
            out_ref[t : t + 1, :] = rate
            col = column(rate)
            kernel_grad = kernel_grad + col[:stations] * load_ref[t, 0:1, :]
            kernel_grad = kernel_grad + col[stations:] * load_ref[t, 1:2, :]
        grad_ref[0:stations, :] = kernel_grad
        grad_ref[stations:, :] = jnp.zeros((8, stations), jnp.float32)

    def run(rv, sq, sv, grads, loads, resp, levels):
        args = [rv, sq, sv, grads, loads, resp]
        for level in range(depth):
            args += list(levels[level])
        return pl.pallas_call(
            kernel,
            out_shape=(
                jax.ShapeDtypeStruct(grads.shape, jnp.float32),
                jax.ShapeDtypeStruct((stations + 8, stations), jnp.float32),
            ),
        )(*args)

    return run


def place(b):
    inner = lax.axis_size("inner")
    return (b % inner) * lax.axis_size("outer") + b // inner


def exchange(x, mask, count):
    return lax.ppermute(x, AXES, [(place(j), place(j ^ mask)) for j in range(count)])


def body(propagator_matrices, smoothed_adjoints, station_loadings, offset_response):
    blocks = propagator_matrices[0]
    grads = smoothed_adjoints[0]
    width = grads.shape[1]
    stations = station_loadings.shape[3]
    count = lax.axis_size("outer") * lax.axis_size("inner")
    me = lax.axis_index("outer") * lax.axis_size("inner") + lax.axis_index("inner")

    leaf_v = vecmat(grads, blocks)
    levels = upsweep(blocks, leaf_v)
    tq, tv = levels[-1]
    tq, tv = tq[0].astype(jnp.float32), tv[0]
    sq = jnp.eye(width, dtype=jnp.float32)
    sv = jnp.zeros((width,), jnp.float32)

    packed = jnp.concatenate([tq, tv[None, :], jnp.zeros((7, width), jnp.float32)], axis=0)
    sv = jnp.zeros((8, width), jnp.float32)
    d = 1
    while 2 * d < count:
        got = exchange(packed, d, count)
        packed, sq, sv = scan_round(d, width)(packed, got, sq, sv)
        d *= 2
    rv = exchange(packed[width:], d, count)
    sizes = [level[0].shape[0] for level in levels]
    length_rates, packed = finish(d, sizes, width, stations)(
        rv, sq, sv, grads, station_loadings[0], offset_response[0], levels
    )
    local_noise = -jnp.sum(length_rates * offset_response[0])
    packed = packed.at[stations, 0].set(local_noise)
    d = 1
    while d < count:
        packed = packed + exchange(packed, d, count)
        d *= 2
    return (length_rates[None], packed[:stations], packed[stations, 0])


def solution(mesh):
    return jax.shard_map(
        body,
        mesh=mesh,
        in_specs=(
            P("outer", "inner", None, None),
            P("outer", "inner", None),
            P("outer", "inner", None, None),
            P("outer", "inner", None),
        ),
        out_specs=(P("outer", "inner", None), P(), P()),
        check_vma=False,
    )
```

```python
import jax
import jax.numpy as jnp
from jax import lax
from jax.experimental import pallas as pl
from jax.experimental.pallas import tpu as pltpu
from jax.sharding import PartitionSpec as P

EXACT = lax.Precision.HIGHEST
AXES = ("inner", "outer")


def vecmat(v, q):
    return jnp.sum(v[:, :, None] * q.astype(jnp.float32), axis=1)


def vecmat_mxu(v, q):
    return jnp.einsum("nj,njk->nk", v, q.astype(jnp.float32), precision=EXACT)


def matmat(later, earlier):
    if later.dtype == jnp.bfloat16 and earlier.dtype == jnp.bfloat16:
        return jnp.einsum("nij,njk->nik", later, earlier, preferred_element_type=jnp.float32)
    return jnp.einsum(
        "nij,njk->nik", later.astype(jnp.float32), earlier.astype(jnp.float32), precision=EXACT
    )


def upsweep(q, v):
    levels = [(q, v)]
    while q.shape[0] > 1:
        n = q.shape[0]
        half = n // 2
        qa, qb = q[0 : 2 * half : 2], q[1 : 2 * half : 2]
        va, vb = v[0 : 2 * half : 2], v[1 : 2 * half : 2]
        nq = matmat(qb, qa)
        nv = vecmat(vb, qa) + va
        if n % 2:
            nq = jnp.concatenate([nq, q[-1:].astype(jnp.float32)], axis=0)
            nv = jnp.concatenate([nv, v[-1:]], axis=0)
        q, v = nq, nv
        levels.append((q, v))
    return levels


def downsweep(levels, incoming):
    m = incoming
    for q, v in reversed(levels[:-1]):
        n = q.shape[0]
        half = n // 2
        upper = m[:half]
        left = vecmat_mxu(upper, q[1 : 2 * half : 2]) + v[1 : 2 * half : 2]
        m_new = jnp.stack([left, upper], axis=1).reshape(2 * half, -1)
        if n % 2:
            m_new = jnp.concatenate([m_new, m[-1:]], axis=0)
        m = m_new
    return m


def scan_round(d, width):
    def kernel(own_ref, got_ref, sq_ref, sv_ref, own_out, sq_out, sv_out):
        me = lax.axis_index("outer") * lax.axis_size("inner") + lax.axis_index("inner")
        lower = (me // d) % 2 == 0
        later = jnp.where(lower, got_ref[...], own_ref[...])
        early_q = jnp.where(lower, own_ref[0:width, :], got_ref[0:width, :])
        early_v = jnp.where(lower, own_ref[width:, :], got_ref[width:, :])
        new_q = jnp.dot(later, early_q, precision=EXACT, preferred_element_type=jnp.float32)
        new_s = jnp.dot(later, sq_ref[...], precision=EXACT, preferred_element_type=jnp.float32)
        own_out[0:width, :] = new_q[0:width]
        own_out[width:, :] = new_q[width:] + early_v
        sq_out[...] = jnp.where(lower, new_s[0:width], sq_ref[...])
        sv_out[...] = jnp.where(lower, new_s[width:] + sv_ref[...], sv_ref[...])

    def run(own, got, sq, sv):
        return pl.pallas_call(
            kernel,
            out_shape=(
                jax.ShapeDtypeStruct(own.shape, jnp.float32),
                jax.ShapeDtypeStruct(sq.shape, jnp.float32),
                jax.ShapeDtypeStruct(sv.shape, jnp.float32),
            ),
        )(own, got, sq, sv)

    return run


def column(row):
    return jnp.broadcast_to(row, (8, row.shape[1])).T[:, 0:1]


def row_times(row, q):
    return jnp.sum(column(row) * q.astype(jnp.float32), axis=0, keepdims=True)


def finish(d, sizes, width, stations, dtypes):
    depth = len(sizes) - 1
    halves = [sizes[level] // 2 for level in range(depth)]

    def kernel(*refs):
        rv_ref, sq_ref, sv_ref, grads_ref, load_ref = refs[:5]
        q_hbm = refs[5 : 5 + depth]
        v_refs = refs[5 + depth : 5 + 2 * depth]
        out_ref, grad_ref = refs[5 + 2 * depth : 7 + 2 * depth]
        bufs = refs[7 + 2 * depth : 7 + 3 * depth]
        sems = refs[7 + 3 * depth]
        copies = {}
        k = 0
        for level in reversed(range(depth)):
            for j in range(halves[level]):
                copy = pltpu.make_async_copy(q_hbm[level].at[2 * j + 1], bufs[level].at[j], sems.at[k])
                copy.start()
                copies[level, j] = copy
                k += 1
        me = lax.axis_index("outer") * lax.axis_size("inner") + lax.axis_index("inner")
        lower = (me // d) % 2 == 0
        sv = sv_ref[0:1, :]
        entering = jnp.where(lower, row_times(rv_ref[0:1, :], sq_ref[...]) + sv, sv)
        rows = [entering]
        for level in reversed(range(depth)):
            v_ref = v_refs[level]
            n = sizes[level]
            new = []
            for j in range(n // 2):
                upper = rows[j]
                copies[level, j].wait()
                new.append(row_times(upper, bufs[level][j]) + v_ref[2 * j + 1 : 2 * j + 2, :])
                new.append(upper)
            if n % 2:
                new.append(rows[-1])
            rows = new
        kernel_grad = jnp.zeros((stations, stations), jnp.float32)
        for t, row in enumerate(rows):
            rate = grads_ref[t : t + 1, :] + row
            out_ref[t : t + 1, :] = rate
            col = column(rate)
            kernel_grad = kernel_grad + col[:stations] * load_ref[t, 0:1, :]
            kernel_grad = kernel_grad + col[stations:] * load_ref[t, 1:2, :]
        grad_ref[0:stations, :] = kernel_grad
        grad_ref[stations:, :] = jnp.zeros((8, stations), jnp.float32)

    def run(rv, sq, sv, grads, loads, levels):
        qs = [levels[level][0] for level in range(depth)]
        vs = [levels[level][1] for level in range(depth)]
        vmem = pl.BlockSpec(memory_space=pltpu.VMEM)
        return pl.pallas_call(
            kernel,
            out_shape=(
                jax.ShapeDtypeStruct(grads.shape, jnp.float32),
                jax.ShapeDtypeStruct((stations + 8, stations), jnp.float32),
            ),
            in_specs=[vmem] * 5 + [pl.BlockSpec(memory_space=pl.ANY)] * depth + [vmem] * depth,
            out_specs=(vmem, vmem),
            scratch_shapes=[pltpu.VMEM((max(halves[level], 1), width, width), dtypes[level]) for level in range(depth)]
            + [pltpu.SemaphoreType.DMA((max(sum(halves), 1),))],
        )(rv, sq, sv, grads, loads, *qs, *vs)

    return run


def place(b):
    inner = lax.axis_size("inner")
    return (b % inner) * lax.axis_size("outer") + b // inner


def exchange(x, mask, count):
    return lax.ppermute(x, AXES, [(place(j), place(j ^ mask)) for j in range(count)])


def body(propagator_matrices, smoothed_adjoints, station_loadings, offset_response):
    blocks = propagator_matrices[0]
    grads = smoothed_adjoints[0]
    width = grads.shape[1]
    stations = station_loadings.shape[3]
    count = lax.axis_size("outer") * lax.axis_size("inner")
    me = lax.axis_index("outer") * lax.axis_size("inner") + lax.axis_index("inner")

    leaf_v = vecmat(grads, blocks)
    levels = upsweep(blocks, leaf_v)
    tq, tv = levels[-1]
    tq, tv = tq[0].astype(jnp.float32), tv[0]
    sq = jnp.eye(width, dtype=jnp.float32)
    sv = jnp.zeros((width,), jnp.float32)

    packed = jnp.concatenate([tq, tv[None, :], jnp.zeros((7, width), jnp.float32)], axis=0)
    sv = jnp.zeros((8, width), jnp.float32)
    d = 1
    while 2 * d < count:
        got = exchange(packed, d, count)
        packed, sq, sv = scan_round(d, width)(packed, got, sq, sv)
        d *= 2
    rv = exchange(packed[width:], d, count)
    sizes = [level[0].shape[0] for level in levels]
    dtypes = [level[0].dtype for level in levels]
    length_rates, packed = finish(d, sizes, width, stations, dtypes)(
        rv, sq, sv, grads, station_loadings[0], levels
    )
    local_noise = -jnp.sum(length_rates * offset_response[0])
    spot = (lax.broadcasted_iota(jnp.int32, packed.shape, 0) == stations) & (
        lax.broadcasted_iota(jnp.int32, packed.shape, 1) == 0
    )
    packed = jnp.where(spot, local_noise, packed)
    d = 1
    while d < count:
        packed = packed + exchange(packed, d, count)
        d *= 2
    return (length_rates[None], packed[:stations], packed[stations, 0])


def solution(mesh):
    return jax.shard_map(
        body,
        mesh=mesh,
        in_specs=(
            P("outer", "inner", None, None),
            P("outer", "inner", None),
            P("outer", "inner", None, None),
            P("outer", "inner", None),
        ),
        out_specs=(P("outer", "inner", None), P(), P()),
        check_vma=False,
    )
```

```python
import jax
import jax.numpy as jnp
from jax import lax
from jax.experimental import pallas as pl
from jax.sharding import PartitionSpec as P

EXACT = lax.Precision.HIGHEST
AXES = ("inner", "outer")


def vecmat(v, q):
    return jnp.sum(v[:, :, None] * q.astype(jnp.float32), axis=1)


def vecmat_mxu(v, q):
    return jnp.einsum("nj,njk->nk", v, q.astype(jnp.float32), precision=EXACT)


def matmat(later, earlier):
    if later.dtype == jnp.bfloat16 and earlier.dtype == jnp.bfloat16:
        return jnp.einsum("nij,njk->nik", later, earlier, preferred_element_type=jnp.float32)
    return jnp.einsum(
        "nij,njk->nik", later.astype(jnp.float32), earlier.astype(jnp.float32), precision=EXACT
    )


def upsweep(q, v):
    levels = [(q, v)]
    while q.shape[0] > 1:
        n = q.shape[0]
        half = n // 2
        qa, qb = q[0 : 2 * half : 2], q[1 : 2 * half : 2]
        va, vb = v[0 : 2 * half : 2], v[1 : 2 * half : 2]
        nq = matmat(qb, qa)
        nv = vecmat(vb, qa) + va
        if n % 2:
            nq = jnp.concatenate([nq, q[-1:].astype(jnp.float32)], axis=0)
            nv = jnp.concatenate([nv, v[-1:]], axis=0)
        q, v = nq, nv
        levels.append((q, v))
    return levels


def downsweep(levels, incoming):
    m = incoming
    for q, v in reversed(levels[:-1]):
        n = q.shape[0]
        half = n // 2
        upper = m[:half]
        left = vecmat_mxu(upper, q[1 : 2 * half : 2]) + v[1 : 2 * half : 2]
        m_new = jnp.stack([left, upper], axis=1).reshape(2 * half, -1)
        if n % 2:
            m_new = jnp.concatenate([m_new, m[-1:]], axis=0)
        m = m_new
    return m


def scan_round(d, width):
    def kernel(own_ref, got_ref, sq_ref, sv_ref, own_out, sq_out, sv_out):
        me = lax.axis_index("outer") * lax.axis_size("inner") + lax.axis_index("inner")
        lower = (me // d) % 2 == 0
        later = jnp.where(lower, got_ref[...], own_ref[...])
        early_q = jnp.where(lower, own_ref[0:width, :], got_ref[0:width, :])
        early_v = jnp.where(lower, own_ref[width:, :], got_ref[width:, :])
        new_q = jnp.dot(later, early_q, precision=EXACT, preferred_element_type=jnp.float32)
        new_s = jnp.dot(later, sq_ref[...], precision=EXACT, preferred_element_type=jnp.float32)
        own_out[0:width, :] = new_q[0:width]
        own_out[width:, :] = new_q[width:] + early_v
        sq_out[...] = jnp.where(lower, new_s[0:width], sq_ref[...])
        sv_out[...] = jnp.where(lower, new_s[width:] + sv_ref[...], sv_ref[...])

    def run(own, got, sq, sv):
        return pl.pallas_call(
            kernel,
            out_shape=(
                jax.ShapeDtypeStruct(own.shape, jnp.float32),
                jax.ShapeDtypeStruct(sq.shape, jnp.float32),
                jax.ShapeDtypeStruct(sv.shape, jnp.float32),
            ),
        )(own, got, sq, sv)

    return run


def column(row):
    return jnp.broadcast_to(row, (8, row.shape[1])).T[:, 0:1]


def row_times(row, q):
    return jnp.sum(column(row) * q.astype(jnp.float32), axis=0, keepdims=True)


def finish(d, sizes, width, stations):
    depth = len(sizes) - 1

    def kernel(*refs):
        rv_ref, sq_ref, sv_ref, grads_ref, load_ref, resp_ref = refs[:6]
        tree = refs[6 : 6 + 2 * depth]
        out_ref, grad_ref = refs[6 + 2 * depth :]
        me = lax.axis_index("outer") * lax.axis_size("inner") + lax.axis_index("inner")
        lower = (me // d) % 2 == 0
        sv = sv_ref[0:1, :]
        entering = jnp.where(lower, row_times(rv_ref[0:1, :], sq_ref[...]) + sv, sv)
        rows = [entering]
        for level in reversed(range(depth)):
            q_ref, v_ref = tree[2 * level], tree[2 * level + 1]
            n = sizes[level]
            new = []
            for j in range(n // 2):
                upper = rows[j]
                new.append(row_times(upper, q_ref[2 * j + 1]) + v_ref[2 * j + 1 : 2 * j + 2, :])
                new.append(upper)
            if n % 2:
                new.append(rows[-1])
            rows = new
        for t, row in enumerate(rows):
            out_ref[t : t + 1, :] = grads_ref[t : t + 1, :] + row
        rates = out_ref[...].T
        kernel_grad = jnp.dot(rates[:stations], load_ref[0], precision=EXACT, preferred_element_type=jnp.float32)
        kernel_grad = kernel_grad + jnp.dot(
            rates[stations:], load_ref[1], precision=EXACT, preferred_element_type=jnp.float32
        )
        grad_ref[0:stations, :] = kernel_grad
        grad_ref[stations:, :] = jnp.zeros((8, stations), jnp.float32)

    def run(rv, sq, sv, grads, loads, resp, levels):
        args = [rv, sq, sv, grads, loads, resp]
        for level in range(depth):
            args += list(levels[level])
        return pl.pallas_call(
            kernel,
            out_shape=(
                jax.ShapeDtypeStruct(grads.shape, jnp.float32),
                jax.ShapeDtypeStruct((stations + 8, stations), jnp.float32),
            ),
        )(*args)

    return run


def place(b):
    inner = lax.axis_size("inner")
    return (b % inner) * lax.axis_size("outer") + b // inner


def exchange(x, mask, count):
    return lax.ppermute(x, AXES, [(place(j), place(j ^ mask)) for j in range(count)])


def body(propagator_matrices, smoothed_adjoints, station_loadings, offset_response):
    blocks = propagator_matrices[0]
    grads = smoothed_adjoints[0]
    width = grads.shape[1]
    stations = station_loadings.shape[3]
    count = lax.axis_size("outer") * lax.axis_size("inner")
    me = lax.axis_index("outer") * lax.axis_size("inner") + lax.axis_index("inner")

    leaf_v = vecmat(grads, blocks)
    levels = upsweep(blocks, leaf_v)
    tq, tv = levels[-1]
    tq, tv = tq[0].astype(jnp.float32), tv[0]
    sq = jnp.eye(width, dtype=jnp.float32)
    sv = jnp.zeros((width,), jnp.float32)

    packed = jnp.concatenate([tq, tv[None, :], jnp.zeros((7, width), jnp.float32)], axis=0)
    sv = jnp.zeros((8, width), jnp.float32)
    d = 1
    while 2 * d < count:
        got = exchange(packed, d, count)
        packed, sq, sv = scan_round(d, width)(packed, got, sq, sv)
        d *= 2
    rv = exchange(packed[width:], d, count)
    sizes = [level[0].shape[0] for level in levels]
    length_rates, packed = finish(d, sizes, width, stations)(
        rv, sq, sv, grads, jnp.transpose(station_loadings[0], (1, 0, 2)), offset_response[0], levels
    )
    local_noise = -jnp.sum(length_rates * offset_response[0])
    packed = packed.at[stations, 0].set(local_noise)
    d = 1
    while d < count:
        packed = packed + exchange(packed, d, count)
        d *= 2
    return (length_rates[None], packed[:stations], packed[stations, 0])


def solution(mesh):
    return jax.shard_map(
        body,
        mesh=mesh,
        in_specs=(
            P("outer", "inner", None, None),
            P("outer", "inner", None),
            P("outer", "inner", None, None),
            P("outer", "inner", None),
        ),
        out_specs=(P("outer", "inner", None), P(), P()),
        check_vma=False,
    )
```

```python
import jax
import jax.numpy as jnp
from jax import lax
from jax.experimental import pallas as pl
from jax.sharding import PartitionSpec as P

EXACT = lax.Precision.HIGHEST
AXES = ("inner", "outer")


def vecmat(v, q):
    return jnp.sum(v[:, :, None] * q.astype(jnp.float32), axis=1)


def split_rows(v):
    first = lax.reduce_precision(v, exponent_bits=8, mantissa_bits=7)
    rest = v - first
    second = lax.reduce_precision(rest, exponent_bits=8, mantissa_bits=7)
    return jnp.stack([first, second, rest - second], axis=1).astype(jnp.bfloat16)


def vecmat_bf16(v, q):
    parts = jnp.einsum("npj,njk->npk", split_rows(v), q, preferred_element_type=jnp.float32)
    return (parts[:, 0] + parts[:, 1]) + parts[:, 2]


def vecmat_mxu(v, q):
    return jnp.einsum("nj,njk->nk", v, q.astype(jnp.float32), precision=EXACT)


def matmat(later, earlier):
    if later.dtype == jnp.bfloat16 and earlier.dtype == jnp.bfloat16:
        return jnp.einsum("nij,njk->nik", later, earlier, preferred_element_type=jnp.float32)
    return jnp.einsum(
        "nij,njk->nik", later.astype(jnp.float32), earlier.astype(jnp.float32), precision=EXACT
    )


def upsweep(q, v):
    levels = [(q, v)]
    while q.shape[0] > 1:
        n = q.shape[0]
        half = n // 2
        qa, qb = q[0 : 2 * half : 2], q[1 : 2 * half : 2]
        va, vb = v[0 : 2 * half : 2], v[1 : 2 * half : 2]
        nq = matmat(qb, qa)
        nv = vecmat(vb, qa) + va
        if n % 2:
            nq = jnp.concatenate([nq, q[-1:].astype(jnp.float32)], axis=0)
            nv = jnp.concatenate([nv, v[-1:]], axis=0)
        q, v = nq, nv
        levels.append((q, v))
    return levels


def downsweep(levels, incoming):
    m = incoming
    for q, v in reversed(levels[:-1]):
        n = q.shape[0]
        half = n // 2
        upper = m[:half]
        left = vecmat_mxu(upper, q[1 : 2 * half : 2]) + v[1 : 2 * half : 2]
        m_new = jnp.stack([left, upper], axis=1).reshape(2 * half, -1)
        if n % 2:
            m_new = jnp.concatenate([m_new, m[-1:]], axis=0)
        m = m_new
    return m


def scan_round(d, width):
    def kernel(own_ref, got_ref, sq_ref, sv_ref, own_out, sq_out, sv_out):
        me = lax.axis_index("outer") * lax.axis_size("inner") + lax.axis_index("inner")
        lower = (me // d) % 2 == 0
        later = jnp.where(lower, got_ref[...], own_ref[...])
        early_q = jnp.where(lower, own_ref[0:width, :], got_ref[0:width, :])
        early_v = jnp.where(lower, own_ref[width:, :], got_ref[width:, :])
        new_q = jnp.dot(later, early_q, precision=EXACT, preferred_element_type=jnp.float32)
        new_s = jnp.dot(later, sq_ref[...], precision=EXACT, preferred_element_type=jnp.float32)
        own_out[0:width, :] = new_q[0:width]
        own_out[width:, :] = new_q[width:] + early_v
        sq_out[...] = jnp.where(lower, new_s[0:width], sq_ref[...])
        sv_out[...] = jnp.where(lower, new_s[width:] + sv_ref[...], sv_ref[...])

    def run(own, got, sq, sv):
        return pl.pallas_call(
            kernel,
            out_shape=(
                jax.ShapeDtypeStruct(own.shape, jnp.float32),
                jax.ShapeDtypeStruct(sq.shape, jnp.float32),
                jax.ShapeDtypeStruct(sv.shape, jnp.float32),
            ),
        )(own, got, sq, sv)

    return run


def column(row):
    return jnp.broadcast_to(row, (8, row.shape[1])).T[:, 0:1]


def row_times(row, q):
    return jnp.sum(column(row) * q.astype(jnp.float32), axis=0, keepdims=True)


def finish(d, sizes, width, stations):
    depth = len(sizes) - 1

    def kernel(*refs):
        rv_ref, sq_ref, sv_ref, grads_ref, load_ref, resp_ref = refs[:6]
        tree = refs[6 : 6 + 2 * depth]
        out_ref, grad_ref = refs[6 + 2 * depth :]
        me = lax.axis_index("outer") * lax.axis_size("inner") + lax.axis_index("inner")
        lower = (me // d) % 2 == 0
        sv = sv_ref[0:1, :]
        entering = jnp.where(lower, row_times(rv_ref[0:1, :], sq_ref[...]) + sv, sv)
        rows = [entering]
        for level in reversed(range(depth)):
            q_ref, v_ref = tree[2 * level], tree[2 * level + 1]
            n = sizes[level]
            new = []
            for j in range(n // 2):
                upper = rows[j]
                new.append(row_times(upper, q_ref[2 * j + 1]) + v_ref[2 * j + 1 : 2 * j + 2, :])
                new.append(upper)
            if n % 2:
                new.append(rows[-1])
            rows = new
        kernel_grad = jnp.zeros((stations, stations), jnp.float32)
        for t, row in enumerate(rows):
            rate = grads_ref[t : t + 1, :] + row
            out_ref[t : t + 1, :] = rate
            col = column(rate)
            kernel_grad = kernel_grad + col[:stations] * load_ref[t, 0:1, :]
            kernel_grad = kernel_grad + col[stations:] * load_ref[t, 1:2, :]
        grad_ref[0:stations, :] = kernel_grad
        grad_ref[stations:, :] = jnp.zeros((8, stations), jnp.float32)

    def run(rv, sq, sv, grads, loads, resp, levels):
        args = [rv, sq, sv, grads, loads, resp]
        for level in range(depth):
            args += list(levels[level])
        return pl.pallas_call(
            kernel,
            out_shape=(
                jax.ShapeDtypeStruct(grads.shape, jnp.float32),
                jax.ShapeDtypeStruct((stations + 8, stations), jnp.float32),
            ),
        )(*args)

    return run


def place(b):
    inner = lax.axis_size("inner")
    return (b % inner) * lax.axis_size("outer") + b // inner


def exchange(x, mask, count):
    return lax.ppermute(x, AXES, [(place(j), place(j ^ mask)) for j in range(count)])


def body(propagator_matrices, smoothed_adjoints, station_loadings, offset_response):
    blocks = propagator_matrices[0]
    grads = smoothed_adjoints[0]
    width = grads.shape[1]
    stations = station_loadings.shape[3]
    count = lax.axis_size("outer") * lax.axis_size("inner")
    me = lax.axis_index("outer") * lax.axis_size("inner") + lax.axis_index("inner")

    leaf_v = vecmat_bf16(grads, blocks)
    levels = upsweep(blocks, leaf_v)
    tq, tv = levels[-1]
    tq, tv = tq[0].astype(jnp.float32), tv[0]
    sq = jnp.eye(width, dtype=jnp.float32)
    sv = jnp.zeros((width,), jnp.float32)

    packed = jnp.concatenate([tq, tv[None, :], jnp.zeros((7, width), jnp.float32)], axis=0)
    sv = jnp.zeros((8, width), jnp.float32)
    d = 1
    while 2 * d < count:
        got = exchange(packed, d, count)
        packed, sq, sv = scan_round(d, width)(packed, got, sq, sv)
        d *= 2
    rv = exchange(packed[width:], d, count)
    sizes = [level[0].shape[0] for level in levels]
    length_rates, packed = finish(d, sizes, width, stations)(
        rv, sq, sv, grads, station_loadings[0], offset_response[0], levels
    )
    local_noise = -jnp.sum(length_rates * offset_response[0])
    packed = packed.at[stations, 0].set(local_noise)
    d = 1
    while d < count:
        packed = packed + exchange(packed, d, count)
        d *= 2
    return (length_rates[None], packed[:stations], packed[stations, 0])


def solution(mesh):
    return jax.shard_map(
        body,
        mesh=mesh,
        in_specs=(
            P("outer", "inner", None, None),
            P("outer", "inner", None),
            P("outer", "inner", None, None),
            P("outer", "inner", None),
        ),
        out_specs=(P("outer", "inner", None), P(), P()),
        check_vma=False,
    )
```

```python
import jax
import jax.numpy as jnp
from jax import lax
from jax.experimental import pallas as pl
from jax.sharding import PartitionSpec as P

EXACT = lax.Precision.HIGHEST
AXES = ("inner", "outer")


def vecmat(v, q):
    return jnp.sum(v[:, :, None] * q.astype(jnp.float32), axis=1)


def vecmat_mxu(v, q):
    return jnp.einsum("nj,njk->nk", v, q.astype(jnp.float32), precision=EXACT)


def matmat(later, earlier):
    if later.dtype == jnp.bfloat16 and earlier.dtype == jnp.bfloat16:
        return jnp.einsum("nij,njk->nik", later, earlier, preferred_element_type=jnp.float32)
    return jnp.einsum(
        "nij,njk->nik", later.astype(jnp.float32), earlier.astype(jnp.float32), precision=EXACT
    )


def upsweep(q, v):
    levels = [(q, v)]
    while q.shape[0] > 1:
        n = q.shape[0]
        half = n // 2
        qa, qb = q[0 : 2 * half : 2], q[1 : 2 * half : 2]
        va, vb = v[0 : 2 * half : 2], v[1 : 2 * half : 2]
        nq = matmat(qb, qa)
        nv = vecmat(vb, qa) + va
        if n % 2:
            nq = jnp.concatenate([nq, q[-1:].astype(jnp.float32)], axis=0)
            nv = jnp.concatenate([nv, v[-1:]], axis=0)
        q, v = nq, nv
        levels.append((q, v))
    return levels


def downsweep(levels, incoming):
    m = incoming
    for q, v in reversed(levels[:-1]):
        n = q.shape[0]
        half = n // 2
        upper = m[:half]
        left = vecmat_mxu(upper, q[1 : 2 * half : 2]) + v[1 : 2 * half : 2]
        m_new = jnp.stack([left, upper], axis=1).reshape(2 * half, -1)
        if n % 2:
            m_new = jnp.concatenate([m_new, m[-1:]], axis=0)
        m = m_new
    return m


def scan_round(d, width):
    def kernel(own_ref, got_ref, sq_ref, sv_ref, own_out, sq_out, sv_out):
        me = lax.axis_index("outer") * lax.axis_size("inner") + lax.axis_index("inner")
        lower = (me // d) % 2 == 0
        later = jnp.where(lower, got_ref[...], own_ref[...])
        early_q = jnp.where(lower, own_ref[0:width, :], got_ref[0:width, :])
        early_v = jnp.where(lower, own_ref[width:, :], got_ref[width:, :])
        right = jnp.concatenate([early_q, sq_ref[...]], axis=1)
        both = jnp.dot(later, right, precision=EXACT, preferred_element_type=jnp.float32)
        own_out[0:width, :] = both[0:width, 0:width]
        own_out[width:, :] = both[width:, 0:width] + early_v
        sq_out[...] = jnp.where(lower, both[0:width, width:], sq_ref[...])
        sv_out[...] = jnp.where(lower, both[width:, width:] + sv_ref[...], sv_ref[...])

    def run(own, got, sq, sv):
        return pl.pallas_call(
            kernel,
            out_shape=(
                jax.ShapeDtypeStruct(own.shape, jnp.float32),
                jax.ShapeDtypeStruct(sq.shape, jnp.float32),
                jax.ShapeDtypeStruct(sv.shape, jnp.float32),
            ),
        )(own, got, sq, sv)

    return run


def column(row):
    return jnp.broadcast_to(row, (8, row.shape[1])).T[:, 0:1]


def row_times(row, q):
    return jnp.sum(column(row) * q.astype(jnp.float32), axis=0, keepdims=True)


def finish(d, sizes, width, stations):
    depth = len(sizes) - 1

    def kernel(*refs):
        rv_ref, sq_ref, sv_ref, grads_ref, load_ref, resp_ref = refs[:6]
        tree = refs[6 : 6 + 2 * depth]
        out_ref, grad_ref = refs[6 + 2 * depth :]
        me = lax.axis_index("outer") * lax.axis_size("inner") + lax.axis_index("inner")
        lower = (me // d) % 2 == 0
        sv = sv_ref[0:1, :]
        entering = jnp.where(lower, row_times(rv_ref[0:1, :], sq_ref[...]) + sv, sv)
        rows = [entering]
        for level in reversed(range(depth)):
            q_ref, v_ref = tree[2 * level], tree[2 * level + 1]
            n = sizes[level]
            new = []
            for j in range(n // 2):
                upper = rows[j]
                new.append(row_times(upper, q_ref[2 * j + 1]) + v_ref[2 * j + 1 : 2 * j + 2, :])
                new.append(upper)
            if n % 2:
                new.append(rows[-1])
            rows = new
        kernel_grad = jnp.zeros((stations, stations), jnp.float32)
        for t, row in enumerate(rows):
            rate = grads_ref[t : t + 1, :] + row
            out_ref[t : t + 1, :] = rate
            col = column(rate)
            kernel_grad = kernel_grad + col[:stations] * load_ref[t, 0:1, :]
            kernel_grad = kernel_grad + col[stations:] * load_ref[t, 1:2, :]
        grad_ref[0:stations, :] = kernel_grad
        grad_ref[stations:, :] = jnp.zeros((8, stations), jnp.float32)

    def run(rv, sq, sv, grads, loads, resp, levels):
        args = [rv, sq, sv, grads, loads, resp]
        for level in range(depth):
            args += list(levels[level])
        return pl.pallas_call(
            kernel,
            out_shape=(
                jax.ShapeDtypeStruct(grads.shape, jnp.float32),
                jax.ShapeDtypeStruct((stations + 8, stations), jnp.float32),
            ),
        )(*args)

    return run


def place(b):
    inner = lax.axis_size("inner")
    return (b % inner) * lax.axis_size("outer") + b // inner


def exchange(x, mask, count):
    return lax.ppermute(x, AXES, [(place(j), place(j ^ mask)) for j in range(count)])


def body(propagator_matrices, smoothed_adjoints, station_loadings, offset_response):
    blocks = propagator_matrices[0]
    grads = smoothed_adjoints[0]
    width = grads.shape[1]
    stations = station_loadings.shape[3]
    count = lax.axis_size("outer") * lax.axis_size("inner")
    me = lax.axis_index("outer") * lax.axis_size("inner") + lax.axis_index("inner")

    leaf_v = vecmat(grads, blocks)
    levels = upsweep(blocks, leaf_v)
    tq, tv = levels[-1]
    tq, tv = tq[0].astype(jnp.float32), tv[0]
    sq = jnp.eye(width, dtype=jnp.float32)
    sv = jnp.zeros((width,), jnp.float32)

    packed = jnp.concatenate([tq, tv[None, :], jnp.zeros((7, width), jnp.float32)], axis=0)
    sv = jnp.zeros((8, width), jnp.float32)
    d = 1
    while 2 * d < count:
        got = exchange(packed, d, count)
        packed, sq, sv = scan_round(d, width)(packed, got, sq, sv)
        d *= 2
    rv = exchange(packed[width:], d, count)
    sizes = [level[0].shape[0] for level in levels]
    length_rates, packed = finish(d, sizes, width, stations)(
        rv, sq, sv, grads, station_loadings[0], offset_response[0], levels
    )
    local_noise = -jnp.sum(length_rates * offset_response[0])
    spot = (lax.broadcasted_iota(jnp.int32, packed.shape, 0) == stations) & (
        lax.broadcasted_iota(jnp.int32, packed.shape, 1) == 0
    )
    packed = jnp.where(spot, local_noise, packed)
    d = 1
    while d < count:
        packed = packed + exchange(packed, d, count)
        d *= 2
    return (length_rates[None], packed[:stations], packed[stations, 0])


def solution(mesh):
    return jax.shard_map(
        body,
        mesh=mesh,
        in_specs=(
            P("outer", "inner", None, None),
            P("outer", "inner", None),
            P("outer", "inner", None, None),
            P("outer", "inner", None),
        ),
        out_specs=(P("outer", "inner", None), P(), P()),
        check_vma=False,
    )
```

```python
import jax
import jax.numpy as jnp
from jax import lax
from jax.experimental import pallas as pl
from jax.sharding import PartitionSpec as P

EXACT = lax.Precision.HIGHEST
AXES = ("inner", "outer")


def vecmat(v, q):
    return jnp.sum(v[:, :, None] * q.astype(jnp.float32), axis=1)


def vecmat_mxu(v, q):
    return jnp.einsum("nj,njk->nk", v, q.astype(jnp.float32), precision=EXACT)


def matmat(later, earlier):
    if later.dtype == jnp.bfloat16 and earlier.dtype == jnp.bfloat16:
        return jnp.einsum("nij,njk->nik", later, earlier, preferred_element_type=jnp.float32)
    return jnp.einsum(
        "nij,njk->nik", later.astype(jnp.float32), earlier.astype(jnp.float32), precision=EXACT
    )


def upsweep(q, v):
    levels = [(q, v)]
    while q.shape[0] > 1:
        n = q.shape[0]
        half = n // 2
        qa, qb = q[0 : 2 * half : 2], q[1 : 2 * half : 2]
        va, vb = v[0 : 2 * half : 2], v[1 : 2 * half : 2]
        nq = matmat(qb, qa)
        nv = vecmat(vb, qa) + va
        if n % 2:
            nq = jnp.concatenate([nq, q[-1:].astype(jnp.float32)], axis=0)
            nv = jnp.concatenate([nv, v[-1:]], axis=0)
        q, v = nq, nv
        levels.append((q, v))
    return levels


def downsweep(levels, incoming):
    m = incoming
    for q, v in reversed(levels[:-1]):
        n = q.shape[0]
        half = n // 2
        upper = m[:half]
        left = vecmat_mxu(upper, q[1 : 2 * half : 2]) + v[1 : 2 * half : 2]
        m_new = jnp.stack([left, upper], axis=1).reshape(2 * half, -1)
        if n % 2:
            m_new = jnp.concatenate([m_new, m[-1:]], axis=0)
        m = m_new
    return m


def scan_round(d, width):
    def kernel(own_ref, got_ref, sq_ref, sv_ref, own_out, sq_out, sv_out):
        me = lax.axis_index("outer") * lax.axis_size("inner") + lax.axis_index("inner")
        lower = (me // d) % 2 == 0
        later = jnp.where(lower, got_ref[...], own_ref[...])
        early_q = jnp.where(lower, own_ref[0:width, :], got_ref[0:width, :])
        early_v = jnp.where(lower, own_ref[width:, :], got_ref[width:, :])
        new_q = jnp.dot(later, early_q, precision=EXACT, preferred_element_type=jnp.float32)
        new_s = jnp.dot(later, sq_ref[...], precision=EXACT, preferred_element_type=jnp.float32)
        own_out[0:width, :] = new_q[0:width]
        own_out[width:, :] = new_q[width:] + early_v
        sq_out[...] = jnp.where(lower, new_s[0:width], sq_ref[...])
        sv_out[...] = jnp.where(lower, new_s[width:] + sv_ref[...], sv_ref[...])

    def run(own, got, sq, sv):
        return pl.pallas_call(
            kernel,
            out_shape=(
                jax.ShapeDtypeStruct(own.shape, jnp.float32),
                jax.ShapeDtypeStruct(sq.shape, jnp.float32),
                jax.ShapeDtypeStruct(sv.shape, jnp.float32),
            ),
        )(own, got, sq, sv)

    return run


def column(row):
    return jnp.broadcast_to(row, (8, row.shape[1])).T[:, 0:1]


def row_times(row, q):
    return jnp.sum(column(row) * q.astype(jnp.float32), axis=0, keepdims=True)


def finish(d, sizes, width, stations):
    depth = len(sizes) - 1

    def kernel(*refs):
        rv_ref, sq_ref, sv_ref, grads_ref, load_ref = refs[:5]
        tree = refs[5 : 5 + 2 * depth]
        out_ref, grad_ref = refs[5 + 2 * depth :]
        me = lax.axis_index("outer") * lax.axis_size("inner") + lax.axis_index("inner")
        lower = (me // d) % 2 == 0
        sv = sv_ref[0:1, :]
        entering = jnp.where(lower, row_times(rv_ref[0:1, :], sq_ref[...]) + sv, sv)
        rows = [entering]
        for level in reversed(range(depth)):
            q_ref, v_ref = tree[2 * level], tree[2 * level + 1]
            n = sizes[level]
            new = []
            for j in range(n // 2):
                upper = rows[j]
                q = q_ref[j, 0] if n % 2 == 0 else q_ref[2 * j + 1]
                new.append(row_times(upper, q) + v_ref[2 * j + 1 : 2 * j + 2, :])
                new.append(upper)
            if n % 2:
                new.append(rows[-1])
            rows = new
        kernel_grad = jnp.zeros((stations, stations), jnp.float32)
        for t, row in enumerate(rows):
            rate = grads_ref[t : t + 1, :] + row
            out_ref[t : t + 1, :] = rate
            col = column(rate)
            kernel_grad = kernel_grad + col[:stations] * load_ref[t, 0:1, :]
            kernel_grad = kernel_grad + col[stations:] * load_ref[t, 1:2, :]
        grad_ref[0:stations, :] = kernel_grad
        grad_ref[stations:, :] = jnp.zeros((8, stations), jnp.float32)

    def whole(x):
        return pl.BlockSpec(x.shape, lambda i, nd=x.ndim: (0,) * nd)

    def run(rv, sq, sv, grads, loads, levels):
        args = [rv, sq, sv, grads, loads]
        specs = [whole(x) for x in args]
        for level in range(depth):
            q, v = levels[level]
            n = sizes[level]
            if n % 2 == 0:
                q = q.reshape((n // 2, 2) + q.shape[1:])
                specs.append(pl.BlockSpec((n // 2, 1) + q.shape[2:], lambda i: (0, 1, 0, 0)))
            else:
                specs.append(whole(q))
            args.append(q)
            specs.append(whole(v))
            args.append(v)
        out_shape = (
            jax.ShapeDtypeStruct(grads.shape, jnp.float32),
            jax.ShapeDtypeStruct((stations + 8, stations), jnp.float32),
        )
        return pl.pallas_call(
            kernel,
            out_shape=out_shape,
            grid=(1,),
            in_specs=specs,
            out_specs=tuple(whole(o) for o in out_shape),
        )(*args)

    return run


def place(b):
    inner = lax.axis_size("inner")
    return (b % inner) * lax.axis_size("outer") + b // inner


def exchange(x, mask, count):
    return lax.ppermute(x, AXES, [(place(j), place(j ^ mask)) for j in range(count)])


def body(propagator_matrices, smoothed_adjoints, station_loadings, offset_response):
    blocks = propagator_matrices[0]
    grads = smoothed_adjoints[0]
    width = grads.shape[1]
    stations = station_loadings.shape[3]
    count = lax.axis_size("outer") * lax.axis_size("inner")
    me = lax.axis_index("outer") * lax.axis_size("inner") + lax.axis_index("inner")

    leaf_v = vecmat(grads, blocks)
    levels = upsweep(blocks, leaf_v)
    tq, tv = levels[-1]
    tq, tv = tq[0].astype(jnp.float32), tv[0]
    sq = jnp.eye(width, dtype=jnp.float32)
    sv = jnp.zeros((width,), jnp.float32)

    packed = jnp.concatenate([tq, tv[None, :], jnp.zeros((7, width), jnp.float32)], axis=0)
    sv = jnp.zeros((8, width), jnp.float32)
    d = 1
    while 2 * d < count:
        got = exchange(packed, d, count)
        packed, sq, sv = scan_round(d, width)(packed, got, sq, sv)
        d *= 2
    rv = exchange(packed[width:], d, count)
    sizes = [level[0].shape[0] for level in levels]
    length_rates, packed = finish(d, sizes, width, stations)(
        rv, sq, sv, grads, station_loadings[0], levels
    )
    local_noise = -jnp.sum(length_rates * offset_response[0])
    packed = packed.at[stations, 0].set(local_noise)
    d = 1
    while d < count:
        packed = packed + exchange(packed, d, count)
        d *= 2
    return (length_rates[None], packed[:stations], packed[stations, 0])


def solution(mesh):
    return jax.shard_map(
        body,
        mesh=mesh,
        in_specs=(
            P("outer", "inner", None, None),
            P("outer", "inner", None),
            P("outer", "inner", None, None),
            P("outer", "inner", None),
        ),
        out_specs=(P("outer", "inner", None), P(), P()),
        check_vma=False,
    )
```

```python
import jax
import jax.numpy as jnp
from jax import lax
from jax.experimental import pallas as pl
from jax.sharding import PartitionSpec as P

EXACT = lax.Precision.HIGHEST
AXES = ("inner", "outer")


def vecmat(v, q):
    return jnp.sum(v[:, :, None] * q.astype(jnp.float32), axis=1)


def vecmat_mxu(v, q):
    return jnp.einsum("nj,njk->nk", v, q.astype(jnp.float32), precision=EXACT)


def matmat(later, earlier):
    if later.dtype == jnp.bfloat16 and earlier.dtype == jnp.bfloat16:
        return jnp.einsum("nij,njk->nik", later, earlier, preferred_element_type=jnp.float32)
    return jnp.einsum(
        "nij,njk->nik", later.astype(jnp.float32), earlier.astype(jnp.float32), precision=EXACT
    )


def upsweep(q, v):
    levels = [(q, v)]
    while q.shape[0] > 1:
        n = q.shape[0]
        half = n // 2
        qa, qb = q[0 : 2 * half : 2], q[1 : 2 * half : 2]
        va, vb = v[0 : 2 * half : 2], v[1 : 2 * half : 2]
        nq = matmat(qb, qa)
        nv = vecmat(vb, qa) + va
        if n % 2:
            nq = jnp.concatenate([nq, q[-1:].astype(jnp.float32)], axis=0)
            nv = jnp.concatenate([nv, v[-1:]], axis=0)
        q, v = nq, nv
        levels.append((q, v))
    return levels


def downsweep(levels, incoming):
    m = incoming
    for q, v in reversed(levels[:-1]):
        n = q.shape[0]
        half = n // 2
        upper = m[:half]
        left = vecmat_mxu(upper, q[1 : 2 * half : 2]) + v[1 : 2 * half : 2]
        m_new = jnp.stack([left, upper], axis=1).reshape(2 * half, -1)
        if n % 2:
            m_new = jnp.concatenate([m_new, m[-1:]], axis=0)
        m = m_new
    return m


def scan_round(d, width):
    def kernel(own_ref, got_ref, sq_ref, sv_ref, own_out, sq_out, sv_out):
        me = lax.axis_index("outer") * lax.axis_size("inner") + lax.axis_index("inner")
        lower = (me // d) % 2 == 0
        later = jnp.where(lower, got_ref[...], own_ref[...])
        early_q = jnp.where(lower, own_ref[0:width, :], got_ref[0:width, :])
        early_v = jnp.where(lower, own_ref[width:, :], got_ref[width:, :])
        new_q = jnp.dot(later, early_q, precision=EXACT, preferred_element_type=jnp.float32)
        new_s = jnp.dot(later, sq_ref[...], precision=EXACT, preferred_element_type=jnp.float32)
        own_out[0:width, :] = new_q[0:width]
        own_out[width:, :] = new_q[width:] + early_v
        sq_out[...] = jnp.where(lower, new_s[0:width], sq_ref[...])
        sv_out[...] = jnp.where(lower, new_s[width:] + sv_ref[...], sv_ref[...])

    def run(own, got, sq, sv):
        return pl.pallas_call(
            kernel,
            out_shape=(
                jax.ShapeDtypeStruct(own.shape, jnp.float32),
                jax.ShapeDtypeStruct(sq.shape, jnp.float32),
                jax.ShapeDtypeStruct(sv.shape, jnp.float32),
            ),
        )(own, got, sq, sv)

    return run


def column(row):
    return jnp.broadcast_to(row, (8, row.shape[1])).T[:, 0:1]


def row_times(row, q):
    return jnp.sum(column(row) * q.astype(jnp.float32), axis=0, keepdims=True)


def finish(d, sizes, width, stations):
    depth = len(sizes) - 1

    def kernel(*refs):
        rv_ref, sq_ref, sv_ref, grads_ref, load_ref = refs[:5]
        tree = refs[5 : 5 + 2 * depth]
        out_ref, grad_ref = refs[5 + 2 * depth :]
        me = lax.axis_index("outer") * lax.axis_size("inner") + lax.axis_index("inner")
        lower = (me // d) % 2 == 0
        sv = sv_ref[0:1, :]
        entering = jnp.where(lower, row_times(rv_ref[0:1, :], sq_ref[...]) + sv, sv)
        rows = [entering]
        for level in reversed(range(depth)):
            q_ref, v_ref = tree[2 * level], tree[2 * level + 1]
            n = sizes[level]
            new = []
            for j in range(n // 2):
                upper = rows[j]
                q = q_ref[j, 0] if n % 2 == 0 else q_ref[2 * j + 1]
                new.append(row_times(upper, q) + v_ref[2 * j + 1 : 2 * j + 2, :])
                new.append(upper)
            if n % 2:
                new.append(rows[-1])
            rows = new
        kernel_grad = jnp.zeros((stations, stations), jnp.float32)
        for t, row in enumerate(rows):
            rate = grads_ref[t : t + 1, :] + row
            out_ref[t : t + 1, :] = rate
            col = column(rate)
            kernel_grad = kernel_grad + col[:stations] * load_ref[t, 0:1, :]
            kernel_grad = kernel_grad + col[stations:] * load_ref[t, 1:2, :]
        grad_ref[0:stations, :] = kernel_grad
        grad_ref[stations:, :] = jnp.zeros((8, stations), jnp.float32)

    def whole(x):
        return pl.BlockSpec(x.shape, lambda i, nd=x.ndim: (0,) * nd)

    def run(rv, sq, sv, grads, loads, levels):
        args = [rv, sq, sv, grads, loads]
        specs = [whole(x) for x in args]
        for level in range(depth):
            q, v = levels[level]
            n = sizes[level]
            if n % 2 == 0:
                q = q.reshape((n // 2, 2) + q.shape[1:])
                specs.append(pl.BlockSpec((n // 2, 1) + q.shape[2:], lambda i: (0, 1, 0, 0)))
            else:
                specs.append(whole(q))
            args.append(q)
            specs.append(whole(v))
            args.append(v)
        out_shape = (
            jax.ShapeDtypeStruct(grads.shape, jnp.float32),
            jax.ShapeDtypeStruct((stations + 8, stations), jnp.float32),
        )
        return pl.pallas_call(
            kernel,
            out_shape=out_shape,
            grid=(1,),
            in_specs=specs,
            out_specs=tuple(whole(o) for o in out_shape),
        )(*args)

    return run


def place(b):
    inner = lax.axis_size("inner")
    return (b % inner) * lax.axis_size("outer") + b // inner


def exchange(x, mask, count):
    return lax.ppermute(x, AXES, [(place(j), place(j ^ mask)) for j in range(count)])


def body(propagator_matrices, smoothed_adjoints, station_loadings, offset_response):
    blocks = propagator_matrices[0]
    grads = smoothed_adjoints[0]
    width = grads.shape[1]
    stations = station_loadings.shape[3]
    count = lax.axis_size("outer") * lax.axis_size("inner")
    me = lax.axis_index("outer") * lax.axis_size("inner") + lax.axis_index("inner")

    leaf_v = vecmat(grads, blocks)
    levels = upsweep(blocks, leaf_v)
    tq, tv = levels[-1]
    tq, tv = tq[0].astype(jnp.float32), tv[0]
    sq = jnp.eye(width, dtype=jnp.float32)
    sv = jnp.zeros((width,), jnp.float32)

    packed = jnp.concatenate([tq, tv[None, :], jnp.zeros((7, width), jnp.float32)], axis=0)
    sv = jnp.zeros((8, width), jnp.float32)
    d = 1
    while 2 * d < count:
        got = exchange(packed, d, count)
        packed, sq, sv = scan_round(d, width)(packed, got, sq, sv)
        d *= 2
    rv = exchange(packed[width:], d, count)
    sizes = [level[0].shape[0] for level in levels]
    length_rates, packed = finish(d, sizes, width, stations)(
        rv, sq, sv, grads, station_loadings[0], levels
    )
    local_noise = -jnp.sum(length_rates * offset_response[0])
    spot = (lax.broadcasted_iota(jnp.int32, packed.shape, 0) == stations) & (
        lax.broadcasted_iota(jnp.int32, packed.shape, 1) == 0
    )
    packed = jnp.where(spot, local_noise, packed)
    d = 1
    while d < count:
        packed = packed + exchange(packed, d, count)
        d *= 2
    return (length_rates[None], packed[:stations], packed[stations, 0])


def solution(mesh):
    return jax.shard_map(
        body,
        mesh=mesh,
        in_specs=(
            P("outer", "inner", None, None),
            P("outer", "inner", None),
            P("outer", "inner", None, None),
            P("outer", "inner", None),
        ),
        out_specs=(P("outer", "inner", None), P(), P()),
        check_vma=False,
    )
```
